32 devices in a mesh: groups: 2 (over x), blk: 16 (over z, y, core).
Axes of the slice: x: 2, y: 2, z: 4, core: 2. Of those that a mesh axis runs over, the one named last changes fastest.
Arguments:
- contacts: float32 [512, 6144], P(('groups', 'blk')), parts along dimension 0, may hold values from 0.1 to 10
- widths: int32 [12288], P('groups'), parts along dimension 0, may hold values from 0 to 3
- masked_bins: int32 [768], P('groups'), parts along dimension 0, may hold values from 0 to 6143, as said below
- row_start: int32 [2], P('groups'), parts along dimension 0, may hold values from 0 to 5888
Outputs:
- correlation: float32 [512, 256], P(('groups', 'blk')), parts along dimension 0
The draws below stay inside these ranges and needn't reach their ends.
There are 2 independent parts, one for each index of `groups`. The reference program is written for one: setup_inputs(seed, part) draws one part's arguments, and reference() takes and returns one part's arrays. A program takes and returns all parts, laid end to end along the dimension named above; each array names one. Nothing has to cross between parts.
Inputs may be any that keep to these rules, and one draw needn't show every extreme that they name: `masked_bins`: distinct bins.
All inputs are finite; a program needn't handle non-finite values.
Results may differ from the reference program's by a relative error of at most 0.00083.
Values may be sent and summed in bfloat16 or wider, within the bound.
No kernel may reach another device: no remote copies, remote signals or barrier semaphores. Data moves between devices by JAX's collectives and lax.ppermute only.
A program may use at most 64 MiB of HBM per device.

```python
import math
import jax
import jax.numpy as jnp
from jax import lax

COLS = 6144
WMAX = 3
NBINS = 256
NMASK = 384


def draw_masked_bins(key, part):
    return jax.random.permutation(key, COLS)[:NMASK].astype(jnp.int32)


def touch_ends(values, key, least, largest):
    longest = values.shape.index(max(values.shape))
    spots = []
    for shift in (0, 1):
        where = [jax.random.randint(jax.random.fold_in(key, axis), (), 0, length) for axis, length in enumerate(values.shape)]
        where[longest] = (where[longest] + shift) % values.shape[longest]
        spots.append(tuple(where))
    return values.at[spots[0]].set(least).at[spots[1]].set(largest)


def steps_of(rng, shape, cuts, low, largest):
    factor_of, own = 1.0, jax.random.fold_in(rng, 6)
    for axis_at, blocks in cuts:
        steps = jnp.exp(jax.random.uniform(jax.random.fold_in(own, axis_at), (blocks,), jnp.float32, low / len(cuts), largest / len(cuts)))
        factor_of = factor_of * jnp.repeat(steps, shape[axis_at] // blocks).reshape([-1 if axis == axis_at else 1 for axis in range(len(shape))])
    return factor_of


def setup_inputs(seed: int = 0, part: int = 0) -> dict:
    splits = jax.random.split(jax.random.key(seed), 5)
    part_splits = jax.random.split(jax.random.fold_in(splits[4], part), 5)
    return {
        "contacts": jnp.clip(jnp.exp(math.log(10.0) - 4.6051702 * jax.random.uniform(part_splits[0], (NBINS, COLS), jnp.float32) ** steps_of(part_splits[0], (NBINS, COLS), ((0, 16),), -0.2, 0.2)), 0.1, 10.0),
        "widths": touch_ends(jax.random.randint(part_splits[1], (COLS,), 0, WMAX + 1), jax.random.fold_in(part_splits[1], 1), 0, WMAX).astype(jnp.int32),
        "masked_bins": draw_masked_bins(jax.random.fold_in(jax.random.fold_in(splits[4], part), 71), part),
        "row_start": jax.random.randint(part_splits[3], (1,), 0, COLS - NBINS + 1).astype(jnp.int32),
    }


def smooth(padded, radius_map):
    rows_here = padded.shape[0] - 2 * WMAX
    col_count = padded.shape[1] - 2 * WMAX
    row_sums = padded[WMAX:WMAX + rows_here]
    smoothed = jnp.zeros((rows_here, col_count), jnp.float32)
    for radius in range(WMAX + 1):
        if radius > 0:
            row_sums = row_sums + padded[WMAX - radius:WMAX - radius + rows_here] + padded[WMAX + radius:WMAX + radius + rows_here]
        box_sums = row_sums[:, WMAX:WMAX + col_count]
        for offset in range(1, radius + 1):
            box_sums = box_sums + row_sums[:, WMAX - offset:WMAX - offset + col_count] + row_sums[:, WMAX + offset:WMAX + offset + col_count]
        smoothed = smoothed + jnp.where(radius_map == radius, box_sums / float((2 * radius + 1) ** 2), 0.0)
    return smoothed

def pair_counts(first_bin, nrows, col_count):
    distance = jnp.arange(col_count, dtype=jnp.int32)
    upper_pairs = jnp.clip(col_count - distance - first_bin, 0, nrows)
    lower_pairs = jnp.clip(first_bin + nrows - distance, 0, nrows)
    pair_total = jnp.where(distance == 0, nrows, upper_pairs + lower_pairs)
    return jnp.maximum(pair_total, 1).astype(jnp.float32)

def normalize(smoothed, expected, distance, kept_rows, kept_cols):
    ratio = smoothed / jnp.take(expected, distance)
    kept_total = jnp.sum(kept_cols)
    row_mean = lax.optimization_barrier(jnp.sum(ratio * kept_cols[None, :], axis=1, keepdims=True)) / kept_total
    centred = (ratio - row_mean) * kept_cols[None, :]
    variance = lax.optimization_barrier(jnp.sum(centred * centred, axis=1, keepdims=True)) / kept_total
    zscores = (centred * lax.rsqrt(variance + 1e-05) * kept_rows[:, None]).astype(jnp.bfloat16)
    return (zscores, kept_total)

def reference(contacts, widths, masked_bins, row_start):
    first_bin = row_start[0]
    row_ids = first_bin + jnp.arange(NBINS, dtype=jnp.int32)
    col_ids = jnp.arange(COLS, dtype=jnp.int32)
    distance = jnp.abs(row_ids[:, None] - col_ids[None, :]).astype(jnp.int32)
    radius_map = jnp.take(widths, distance)
    padded = jnp.pad(contacts, WMAX)
    smoothed = smooth(padded, radius_map)
    diag_total = jax.ops.segment_sum(smoothed.ravel(), distance.ravel(), num_segments=COLS)
    expected = diag_total / pair_counts(first_bin, NBINS, COLS)
    kept_bins = jnp.ones((COLS,), jnp.float32).at[masked_bins].set(0.0)
    kept_rows = lax.dynamic_slice_in_dim(kept_bins, first_bin, NBINS)
    zscores, kept_total = normalize(smoothed, expected, distance, kept_rows, kept_bins)
    wide = zscores.astype(jnp.float32)
    return jnp.dot(wide, wide.T, preferred_element_type=jnp.float32) / kept_total
```

```python
import jax
import jax.numpy as jnp
from jax import lax
from jax.sharding import PartitionSpec as P

WMAX = 3


def with_halo(cells, sides, width):
    for axis, dim in sides:
        count = lax.axis_size(axis)
        ends = count - 1
        head = lax.slice_in_dim(cells, 0, width, axis=dim)
        tail = lax.slice_in_dim(cells, cells.shape[dim] - width, cells.shape[dim], axis=dim)
        cells = jnp.concatenate(
            [
                lax.ppermute(tail, axis, [(i, (i + 1) % count) for i in range(ends)]),
                cells,
                lax.ppermute(head, axis, [((i + 1) % count, i) for i in range(ends)]),
            ],
            axis=dim,
        )
    return cells


def smooth(padded, radius_map):
    rows_here = padded.shape[0] - 2 * WMAX
    col_count = padded.shape[1] - 2 * WMAX
    row_sums = padded[WMAX : WMAX + rows_here]
    smoothed = jnp.zeros((rows_here, col_count), jnp.float32)
    for radius in range(WMAX + 1):
        if radius > 0:
            row_sums = (
                row_sums
                + padded[WMAX - radius : WMAX - radius + rows_here]
                + padded[WMAX + radius : WMAX + radius + rows_here]
            )
        box_sums = row_sums[:, WMAX : WMAX + col_count]
        for offset in range(1, radius + 1):
            box_sums = (
                box_sums
                + row_sums[:, WMAX - offset : WMAX - offset + col_count]
                + row_sums[:, WMAX + offset : WMAX + offset + col_count]
            )
        smoothed = smoothed + jnp.where(
            radius_map == radius, box_sums / float((2 * radius + 1) ** 2), 0.0
        )
    return smoothed


def pair_counts(first_bin, nrows, col_count):
    distance = jnp.arange(col_count, dtype=jnp.int32)
    upper_pairs = jnp.clip(col_count - distance - first_bin, 0, nrows)
    lower_pairs = jnp.clip(first_bin + nrows - distance, 0, nrows)
    pair_total = jnp.where(distance == 0, nrows, upper_pairs + lower_pairs)
    return jnp.maximum(pair_total, 1).astype(jnp.float32)


def mirrored_table(table):
    return jnp.concatenate([table[1:][::-1], table])


def skewed_map(table, window_first, rows_here, col_count):
    span = col_count + rows_here - 1
    window = lax.dynamic_slice_in_dim(mirrored_table(table), window_first, span)
    tiled = jnp.tile(window, rows_here + 1)[: rows_here * (span + 1)]
    shifted = tiled.reshape(rows_here, span + 1)[:, :col_count]
    return shifted[::-1]


def diagonal_totals(smoothed, window_first):
    rows_here = smoothed.shape[0]
    col_count = smoothed.shape[1]
    span = col_count + rows_here - 1
    flipped = jnp.pad(smoothed[::-1], ((0, 0), (0, rows_here)))
    flat = flipped.reshape(rows_here * (col_count + rows_here))[: rows_here * span]
    offsets = jnp.sum(flat.reshape(rows_here, span), axis=0)
    spread = lax.dynamic_update_slice_in_dim(
        jnp.zeros((2 * col_count - 1,), jnp.float32), offsets, window_first, 0
    )
    lower = jnp.concatenate([jnp.zeros((1,), jnp.float32), spread[: col_count - 1][::-1]])
    return spread[col_count - 1 :] + lower


def normalize(smoothed, expected_map, kept_rows, kept_cols):
    ratio = smoothed / expected_map
    kept_total = jnp.sum(kept_cols)
    row_mean = jnp.sum(ratio * kept_cols[None, :], axis=1, keepdims=True) / kept_total
    centred = (ratio - row_mean) * kept_cols[None, :]
    variance = jnp.sum(centred * centred, axis=1, keepdims=True) / kept_total
    zscores = (centred * lax.rsqrt(variance + 1e-05) * kept_rows[:, None]).astype(jnp.bfloat16)
    return (zscores, kept_total)


def cross_block(left, right):
    return lax.dot_general(
        left, right, (((1,), (1,)), ((), ())), preferred_element_type=jnp.float32
    )


def tree_sum(values, axis):
    count = lax.axis_size(axis)
    if count & (count - 1):
        return lax.psum(values, axis)
    step = 1
    while step < count:
        values = values + lax.ppermute(values, axis, [(i, i ^ step) for i in range(count)])
        step *= 2
    return values


def gram_rows(zscores, axis):
    blocks = lax.axis_size(axis)
    rows_here = zscores.shape[0]
    columns = lax.all_to_all(zscores, axis, 1, 0, tiled=True)
    partial = cross_block(columns, columns)
    pieces = lax.all_to_all(partial, axis, 0, 0, tiled=True)
    return jnp.sum(pieces.reshape(blocks, rows_here, pieces.shape[1]), axis=0)


def shards(contacts, widths, masked_bins, row_start):
    blocks = lax.axis_size("blk")
    position = lax.axis_index("blk")
    rows_here = contacts.shape[0]
    col_count = contacts.shape[1]
    nbins = rows_here * blocks
    first_row = position * rows_here
    first_bin = row_start[0]
    window_first = col_count - 1 - (first_bin + first_row + rows_here - 1)
    radius_map = skewed_map(widths, window_first, rows_here, col_count)
    padded_rows = with_halo(contacts, (("blk", 0),), WMAX)
    padded = jnp.pad(padded_rows, ((0, 0), (WMAX, WMAX)))
    smoothed = smooth(padded, radius_map)
    local_total = diagonal_totals(smoothed, window_first)
    denominator = pair_counts(first_bin, nbins, col_count)
    expected = tree_sum(local_total, "blk") / denominator
    expected_map = skewed_map(expected, window_first, rows_here, col_count)
    kept_bins = jnp.ones((col_count,), jnp.float32).at[masked_bins].set(0.0)
    kept_rows = lax.dynamic_slice_in_dim(kept_bins, first_bin + first_row, rows_here)
    zscores, kept_total = normalize(smoothed, expected_map, kept_rows, kept_bins)
    return gram_rows(zscores, "blk") / kept_total


def solution(mesh):
    return jax.shard_map(
        shards,
        mesh=mesh,
        in_specs=(P(("groups", "blk"), None), P("groups"), P("groups"), P("groups")),
        out_specs=P(("groups", "blk"), None),
        check_vma=False,
    )
```

```python
import jax
import jax.numpy as jnp
from jax import lax
from jax.sharding import PartitionSpec as P

WMAX = 3


def with_halo(cells, sides, width):
    for axis, dim in sides:
        count = lax.axis_size(axis)
        ends = count - 1
        head = lax.slice_in_dim(cells, 0, width, axis=dim)
        tail = lax.slice_in_dim(cells, cells.shape[dim] - width, cells.shape[dim], axis=dim)
        cells = jnp.concatenate(
            [
                lax.ppermute(tail, axis, [(i, (i + 1) % count) for i in range(ends)]),
                cells,
                lax.ppermute(head, axis, [((i + 1) % count, i) for i in range(ends)]),
            ],
            axis=dim,
        )
    return cells


def smooth(padded, radius_map):
    rows_here = padded.shape[0] - 2 * WMAX
    col_count = padded.shape[1] - 2 * WMAX
    row_sums = padded[WMAX : WMAX + rows_here]
    smoothed = jnp.zeros((rows_here, col_count), jnp.float32)
    for radius in range(WMAX + 1):
        if radius > 0:
            row_sums = (
                row_sums
                + padded[WMAX - radius : WMAX - radius + rows_here]
                + padded[WMAX + radius : WMAX + radius + rows_here]
            )
        box_sums = row_sums[:, WMAX : WMAX + col_count]
        for offset in range(1, radius + 1):
            box_sums = (
                box_sums
                + row_sums[:, WMAX - offset : WMAX - offset + col_count]
                + row_sums[:, WMAX + offset : WMAX + offset + col_count]
            )
        smoothed = smoothed + jnp.where(
            radius_map == radius, box_sums / float((2 * radius + 1) ** 2), 0.0
        )
    return smoothed


def pair_counts(first_bin, nrows, col_count):
    distance = jnp.arange(col_count, dtype=jnp.int32)
    upper_pairs = jnp.clip(col_count - distance - first_bin, 0, nrows)
    lower_pairs = jnp.clip(first_bin + nrows - distance, 0, nrows)
    pair_total = jnp.where(distance == 0, nrows, upper_pairs + lower_pairs)
    return jnp.maximum(pair_total, 1).astype(jnp.float32)


def mirrored_table(table, margin=0):
    mirrored = jnp.concatenate([table[1:][::-1], table])
    return jnp.pad(mirrored, margin, mode="edge")


def skewed_map(table, window_first, rows_here, col_count, margin=0):
    span = col_count + rows_here - 1
    window = lax.dynamic_slice_in_dim(
        mirrored_table(table, margin), window_first + margin, span
    )
    tiled = jnp.tile(window, rows_here + 1)[: rows_here * (span + 1)]
    shifted = tiled.reshape(rows_here, span + 1)[:, :col_count]
    return shifted[::-1]


def diagonal_totals(smoothed, window_first, margin=0):
    rows_here = smoothed.shape[0]
    col_count = smoothed.shape[1]
    span = col_count + rows_here - 1
    flipped = jnp.pad(smoothed[::-1], ((0, 0), (0, rows_here)))
    flat = flipped.reshape(rows_here * (col_count + rows_here))[: rows_here * span]
    offsets = jnp.sum(flat.reshape(rows_here, span), axis=0)
    spread = lax.dynamic_update_slice_in_dim(
        jnp.zeros((2 * col_count - 1 + 2 * margin,), jnp.float32),
        offsets,
        window_first + margin,
        0,
    )[margin : margin + 2 * col_count - 1]
    lower = jnp.concatenate([jnp.zeros((1,), jnp.float32), spread[: col_count - 1][::-1]])
    return spread[col_count - 1 :] + lower


def normalize(smoothed, expected_map, kept_rows, kept_cols):
    ratio = smoothed / expected_map
    kept_total = jnp.sum(kept_cols)
    row_mean = jnp.sum(ratio * kept_cols[None, :], axis=1, keepdims=True) / kept_total
    centred = (ratio - row_mean) * kept_cols[None, :]
    variance = jnp.sum(centred * centred, axis=1, keepdims=True) / kept_total
    zscores = (centred * lax.rsqrt(variance + 1e-05) * kept_rows[:, None]).astype(jnp.bfloat16)
    return (zscores, kept_total)


def cross_block(left, right):
    return lax.dot_general(
        left, right, (((1,), (1,)), ((), ())), preferred_element_type=jnp.float32
    )


def tree_sum(values, axis):
    count = lax.axis_size(axis)
    if count & (count - 1):
        return lax.psum(values, axis)
    step = 1
    while step < count:
        values = values + lax.ppermute(values, axis, [(i, i ^ step) for i in range(count)])
        step *= 2
    return values


def gram_rows(zscores, axis):
    blocks = lax.axis_size(axis)
    rows_here = zscores.shape[0]
    columns = lax.all_to_all(zscores, axis, 1, 0, tiled=True)
    partial = cross_block(columns, columns)
    pieces = lax.all_to_all(partial, axis, 0, 0, tiled=True)
    return jnp.sum(pieces.reshape(blocks, rows_here, pieces.shape[1]), axis=0)


def shards(contacts, widths, masked_bins, row_start):
    blocks = lax.axis_size("blk")
    position = lax.axis_index("blk")
    rows_here = contacts.shape[0]
    col_count = contacts.shape[1]
    nbins = rows_here * blocks
    first_row = position * rows_here
    first_bin = row_start[0]
    window_first = col_count - 1 - (first_bin + first_row + rows_here - 1)
    wide_rows = rows_here + 2 * WMAX
    wide_first = window_first - WMAX
    wide_radius = skewed_map(widths, wide_first, wide_rows, col_count, WMAX)
    own = jnp.pad(contacts, ((2 * WMAX, 2 * WMAX), (WMAX, WMAX)))
    target = first_row - WMAX + jnp.arange(wide_rows, dtype=jnp.int32)
    inside = (target >= 0) & (target < nbins)
    own_part = jnp.where(inside[:, None], smooth(own, wide_radius), 0.0)
    local_total = diagonal_totals(own_part, wide_first, WMAX)
    radius_map = skewed_map(widths, window_first, rows_here, col_count)
    padded_rows = with_halo(contacts, (("blk", 0),), WMAX)
    padded = jnp.pad(padded_rows, ((0, 0), (WMAX, WMAX)))
    smoothed = smooth(padded, radius_map)
    denominator = pair_counts(first_bin, nbins, col_count)
    expected = tree_sum(local_total, "blk") / denominator
    expected_map = skewed_map(expected, window_first, rows_here, col_count)
    kept_bins = jnp.ones((col_count,), jnp.float32).at[masked_bins].set(0.0)
    kept_rows = lax.dynamic_slice_in_dim(kept_bins, first_bin + first_row, rows_here)
    zscores, kept_total = normalize(smoothed, expected_map, kept_rows, kept_bins)
    return gram_rows(zscores, "blk") / kept_total


def solution(mesh):
    return jax.shard_map(
        shards,
        mesh=mesh,
        in_specs=(P(("groups", "blk"), None), P("groups"), P("groups"), P("groups")),
        out_specs=P(("groups", "blk"), None),
        check_vma=False,
    )
```

```python
import jax
import jax.numpy as jnp
from jax import lax
from jax.experimental import pallas as pl
from jax.experimental.pallas import tpu as pltpu
from jax.sharding import PartitionSpec as P

WMAX = 3
LANE = 128

def smooth_kernel(xp_ref, w_ref, s_ref, tot_ref):
    rows, cols = s_ref.shape
    width = w_ref.shape[1]
    skew = pltpu.roll(jnp.broadcast_to(w_ref[...], (rows, width)), width - (rows - 1), 1, stride=1, stride_axis=0)
    radius = skew[:, :cols]
    col = lax.broadcasted_iota(jnp.int32, (rows, cols), 1)
    row_sums = xp_ref[WMAX:WMAX + rows, :]
    smoothed = jnp.zeros((rows, cols), jnp.float32)
    for r in range(WMAX + 1):
        if r > 0:
            row_sums = row_sums + xp_ref[WMAX - r:WMAX - r + rows, :] + xp_ref[WMAX + r:WMAX + r + rows, :]
        box = row_sums
        for o in range(1, r + 1):
            box = (box + jnp.where(col >= o, pltpu.roll(row_sums, o, 1), 0.0)
                   + jnp.where(col < cols - o, pltpu.roll(row_sums, cols - o, 1), 0.0))
        smoothed = smoothed + jnp.where(radius == float(r), box / float((2 * r + 1) ** 2), 0.0)
    s_ref[...] = smoothed
    placed = jnp.concatenate([jnp.zeros((rows, width - cols), jnp.float32), smoothed], axis=1)
    total = placed[0:1, :]
    for i in range(1, rows):
        total = total + pltpu.roll(placed[i:i + 1, :], width - i, 1)
    tot_ref[...] = total

def smooth_call(xp, wrow, rows):
    cols = xp.shape[1]
    return pl.pallas_call(
        smooth_kernel,
        out_shape=(jax.ShapeDtypeStruct((rows, cols), jnp.float32), jax.ShapeDtypeStruct((1, wrow.shape[1]), jnp.float32)),
        in_specs=[pl.BlockSpec(memory_space=pltpu.VMEM)] * 2,
        out_specs=(pl.BlockSpec(memory_space=pltpu.VMEM),) * 2,
    )(xp, wrow)

def zscore_kernel(s_ref, e_ref, keep_ref, krow_ref, kt_ref, z_ref):
    rows, cols = s_ref.shape
    width = e_ref.shape[1]
    skew = pltpu.roll(jnp.broadcast_to(e_ref[...], (rows, width)), width - (rows - 1), 1, stride=1, stride_axis=0)
    ratio = s_ref[...] / skew[:, :cols]
    keep = keep_ref[...]
    kt = kt_ref[...]
    mean = jnp.sum(ratio * keep, axis=1, keepdims=True) / kt
    centred = (ratio - mean) * keep
    var = jnp.sum(centred * centred, axis=1, keepdims=True) / kt
    z_ref[...] = (centred * lax.rsqrt(var + 1e-05) * krow_ref[...]).astype(z_ref.dtype)

def zscore_call(s, erow, keep, krow, kt):
    return pl.pallas_call(
        zscore_kernel,
        out_shape=jax.ShapeDtypeStruct(s.shape, jnp.bfloat16),
        in_specs=[pl.BlockSpec(memory_space=pltpu.VMEM)] * 5,
        out_specs=pl.BlockSpec(memory_space=pltpu.VMEM),
    )(s, erow, keep, krow, kt)


def with_halo(cells, sides, width):
    for axis, dim in sides:
        count = lax.axis_size(axis)
        ends = count - 1
        head = lax.slice_in_dim(cells, 0, width, axis=dim)
        tail = lax.slice_in_dim(cells, cells.shape[dim] - width, cells.shape[dim], axis=dim)
        cells = jnp.concatenate(
            [
                lax.ppermute(tail, axis, [(i, (i + 1) % count) for i in range(ends)]),
                cells,
                lax.ppermute(head, axis, [((i + 1) % count, i) for i in range(ends)]),
            ],
            axis=dim,
        )
    return cells


def smooth(padded, radius_map):
    rows_here = padded.shape[0] - 2 * WMAX
    col_count = padded.shape[1] - 2 * WMAX
    row_sums = padded[WMAX : WMAX + rows_here]
    smoothed = jnp.zeros((rows_here, col_count), jnp.float32)
    for radius in range(WMAX + 1):
        if radius > 0:
            row_sums = (
                row_sums
                + padded[WMAX - radius : WMAX - radius + rows_here]
                + padded[WMAX + radius : WMAX + radius + rows_here]
            )
        box_sums = row_sums[:, WMAX : WMAX + col_count]
        for offset in range(1, radius + 1):
            box_sums = (
                box_sums
                + row_sums[:, WMAX - offset : WMAX - offset + col_count]
                + row_sums[:, WMAX + offset : WMAX + offset + col_count]
            )
        smoothed = smoothed + jnp.where(
            radius_map == radius, box_sums / float((2 * radius + 1) ** 2), 0.0
        )
    return smoothed


def pair_counts(first_bin, nrows, col_count):
    distance = jnp.arange(col_count, dtype=jnp.int32)
    upper_pairs = jnp.clip(col_count - distance - first_bin, 0, nrows)
    lower_pairs = jnp.clip(first_bin + nrows - distance, 0, nrows)
    pair_total = jnp.where(distance == 0, nrows, upper_pairs + lower_pairs)
    return jnp.maximum(pair_total, 1).astype(jnp.float32)


def mirrored_table(table):
    return jnp.concatenate([table[1:][::-1], table])


def skewed_map(table, window_first, rows_here, col_count):
    span = col_count + rows_here - 1
    window = lax.dynamic_slice_in_dim(mirrored_table(table), window_first, span)
    tiled = jnp.tile(window, rows_here + 1)[: rows_here * (span + 1)]
    shifted = tiled.reshape(rows_here, span + 1)[:, :col_count]
    return shifted[::-1]


def diagonal_totals(smoothed, window_first):
    rows_here = smoothed.shape[0]
    col_count = smoothed.shape[1]
    span = col_count + rows_here - 1
    flipped = jnp.pad(smoothed[::-1], ((0, 0), (0, rows_here)))
    flat = flipped.reshape(rows_here * (col_count + rows_here))[: rows_here * span]
    offsets = jnp.sum(flat.reshape(rows_here, span), axis=0)
    spread = lax.dynamic_update_slice_in_dim(
        jnp.zeros((2 * col_count - 1,), jnp.float32), offsets, window_first, 0
    )
    lower = jnp.concatenate([jnp.zeros((1,), jnp.float32), spread[: col_count - 1][::-1]])
    return spread[col_count - 1 :] + lower


def normalize(smoothed, expected_map, kept_rows, kept_cols):
    ratio = smoothed / expected_map
    kept_total = jnp.sum(kept_cols)
    row_mean = jnp.sum(ratio * kept_cols[None, :], axis=1, keepdims=True) / kept_total
    centred = (ratio - row_mean) * kept_cols[None, :]
    variance = jnp.sum(centred * centred, axis=1, keepdims=True) / kept_total
    zscores = (centred * lax.rsqrt(variance + 1e-05) * kept_rows[:, None]).astype(jnp.bfloat16)
    return (zscores, kept_total)


def cross_block(left, right):
    return lax.dot_general(
        left, right, (((1,), (1,)), ((), ())), preferred_element_type=jnp.float32
    )


def tree_sum(values, axis):
    count = lax.axis_size(axis)
    if count & (count - 1):
        return lax.psum(values, axis)
    step = 1
    while step < count:
        values = values + lax.ppermute(values, axis, [(i, i ^ step) for i in range(count)])
        step *= 2
    return values


def gram_rows(zscores, axis):
    blocks = lax.axis_size(axis)
    rows_here = zscores.shape[0]
    columns = lax.all_to_all(zscores, axis, 1, 0, tiled=True)
    partial = cross_block(columns, columns)
    pieces = lax.all_to_all(partial, axis, 0, 0, tiled=True)
    return jnp.sum(pieces.reshape(blocks, rows_here, pieces.shape[1]), axis=0)


def window_row(table, window_first, width):
    mirrored = jnp.pad(mirrored_table(table.astype(jnp.float32)), (0, width))
    return lax.dynamic_slice_in_dim(mirrored, window_first, width)[None]


def signed_totals(totals, first_bin, col_count):
    width = totals.shape[1]
    spread = lax.dynamic_update_slice_in_dim(
        jnp.zeros((2 * col_count - 1 + 2 * width,), jnp.float32),
        totals[0],
        col_count - 1 - (width - col_count) - first_bin + width,
        0,
    )[width : width + 2 * col_count - 1]
    lower = jnp.concatenate([jnp.zeros((1,), jnp.float32), spread[: col_count - 1][::-1]])
    return spread[col_count - 1 :] + lower


def shards(contacts, widths, masked_bins, row_start):
    blocks = lax.axis_size("blk")
    position = lax.axis_index("blk")
    rows_here = contacts.shape[0]
    col_count = contacts.shape[1]
    nbins = rows_here * blocks
    first_row = position * rows_here
    first_bin = row_start[0]
    window_first = col_count - 1 - (first_bin + first_row + rows_here - 1)
    width = col_count + LANE
    padded_rows = with_halo(contacts, (("blk", 0),), WMAX)
    extra = -padded_rows.shape[0] % 8
    padded = jnp.pad(padded_rows, ((0, extra), (0, 0)))
    smoothed, totals = smooth_call(padded, window_row(widths, window_first, width), rows_here)
    local_total = signed_totals(totals, first_bin + first_row, col_count)
    denominator = pair_counts(first_bin, nbins, col_count)
    expected = tree_sum(local_total, "blk") / denominator
    kept_bins = jnp.ones((col_count,), jnp.float32).at[masked_bins].set(0.0)
    kept_rows = lax.dynamic_slice_in_dim(kept_bins, first_bin + first_row, rows_here)
    kept_total = jnp.sum(kept_bins)
    zscores = zscore_call(
        smoothed,
        window_row(expected, window_first, width),
        kept_bins[None],
        kept_rows[:, None],
        kept_total.reshape(1, 1),
    )
    return gram_rows(zscores, "blk") / kept_total


def solution(mesh):
    return jax.shard_map(
        shards,
        mesh=mesh,
        in_specs=(P(("groups", "blk"), None), P("groups"), P("groups"), P("groups")),
        out_specs=P(("groups", "blk"), None),
        check_vma=False,
    )
```

```python
import jax
import jax.numpy as jnp
from jax import lax
from jax.sharding import PartitionSpec as P

WMAX = 3


def with_halo(cells, sides, width):
    for axis, dim in sides:
        count = lax.axis_size(axis)
        ends = count - 1
        head = lax.slice_in_dim(cells, 0, width, axis=dim)
        tail = lax.slice_in_dim(cells, cells.shape[dim] - width, cells.shape[dim], axis=dim)
        cells = jnp.concatenate(
            [
                lax.ppermute(tail, axis, [(i, (i + 1) % count) for i in range(ends)]),
                cells,
                lax.ppermute(head, axis, [((i + 1) % count, i) for i in range(ends)]),
            ],
            axis=dim,
        )
    return cells


def smooth(padded, radius_map):
    rows_here = padded.shape[0] - 2 * WMAX
    col_count = padded.shape[1] - 2 * WMAX
    row_sums = padded[WMAX : WMAX + rows_here]
    smoothed = jnp.zeros((rows_here, col_count), jnp.float32)
    for radius in range(WMAX + 1):
        if radius > 0:
            row_sums = (
                row_sums
                + padded[WMAX - radius : WMAX - radius + rows_here]
                + padded[WMAX + radius : WMAX + radius + rows_here]
            )
        box_sums = row_sums[:, WMAX : WMAX + col_count]
        for offset in range(1, radius + 1):
            box_sums = (
                box_sums
                + row_sums[:, WMAX - offset : WMAX - offset + col_count]
                + row_sums[:, WMAX + offset : WMAX + offset + col_count]
            )
        smoothed = smoothed + jnp.where(
            radius_map == radius, box_sums / float((2 * radius + 1) ** 2), 0.0
        )
    return smoothed


def pair_counts(first_bin, nrows, col_count):
    distance = jnp.arange(col_count, dtype=jnp.int32)
    upper_pairs = jnp.clip(col_count - distance - first_bin, 0, nrows)
    lower_pairs = jnp.clip(first_bin + nrows - distance, 0, nrows)
    pair_total = jnp.where(distance == 0, nrows, upper_pairs + lower_pairs)
    return jnp.maximum(pair_total, 1).astype(jnp.float32)


def mirrored_table(table):
    return jnp.concatenate([table[1:][::-1], table])


def skewed_map(table, window_first, rows_here, col_count):
    span = col_count + rows_here - 1
    window = lax.dynamic_slice_in_dim(mirrored_table(table), window_first, span)
    tiled = jnp.tile(window, rows_here + 1)
    flat = tiled[rows_here - 1 : rows_here - 1 + rows_here * (span - 1)]
    return flat.reshape(rows_here, span - 1)[:, :col_count]


def diagonal_totals(smoothed, window_first):
    rows_here = smoothed.shape[0]
    col_count = smoothed.shape[1]
    span = col_count + rows_here - 1
    placed = jnp.pad(smoothed, ((0, 0), (rows_here - 1, 0)))
    flat = jnp.pad(placed.reshape(rows_here * span), (0, rows_here))
    offsets = jnp.sum(flat.reshape(rows_here, span + 1), axis=0)[:span]
    spread = lax.dynamic_update_slice_in_dim(
        jnp.zeros((2 * col_count - 1,), jnp.float32), offsets, window_first, 0
    )
    lower = jnp.concatenate([jnp.zeros((1,), jnp.float32), spread[: col_count - 1][::-1]])
    return spread[col_count - 1 :] + lower


def normalize(smoothed, expected_map, kept_rows, kept_cols, kept_total):
    ratio = smoothed / expected_map
    row_mean = jnp.sum(ratio * kept_cols[None, :], axis=1, keepdims=True) / kept_total
    centred = (ratio - row_mean) * kept_cols[None, :]
    variance = jnp.sum(centred * centred, axis=1, keepdims=True) / kept_total
    return (centred * lax.rsqrt(variance + 1e-05) * kept_rows[:, None]).astype(jnp.bfloat16)


def cross_block(left, right):
    return lax.dot_general(
        left, right, (((1,), (1,)), ((), ())), preferred_element_type=jnp.float32
    )


def tree_sum(values, axis):
    count = lax.axis_size(axis)
    if count & (count - 1):
        return lax.psum(values, axis)
    step = 1
    while step < count:
        values = values + lax.ppermute(values, axis, [(i, i ^ step) for i in range(count)])
        step *= 2
    return values


def gram_rows(zscores, axis):
    blocks = lax.axis_size(axis)
    rows_here = zscores.shape[0]
    columns = lax.all_to_all(zscores, axis, 1, 0, tiled=True)
    partial = cross_block(columns, columns)
    pieces = lax.all_to_all(partial, axis, 0, 0, tiled=True)
    return jnp.sum(pieces.reshape(blocks, rows_here, pieces.shape[1]), axis=0)


def shards(contacts, widths, masked_bins, row_start):
    blocks = lax.axis_size("blk")
    position = lax.axis_index("blk")
    rows_here = contacts.shape[0]
    col_count = contacts.shape[1]
    nbins = rows_here * blocks
    first_row = position * rows_here
    first_bin = row_start[0]
    window_first = col_count - 1 - (first_bin + first_row + rows_here - 1)
    radius_map = skewed_map(widths, window_first, rows_here, col_count)
    padded_rows = with_halo(contacts, (("blk", 0),), WMAX)
    padded = jnp.pad(padded_rows, ((0, 0), (WMAX, WMAX)))
    smoothed = smooth(padded, radius_map)
    local_total = diagonal_totals(smoothed, window_first)
    denominator = pair_counts(first_bin, nbins, col_count)
    expected = tree_sum(local_total, "blk") / denominator
    expected_map = skewed_map(expected, window_first, rows_here, col_count)
    kept_bins = jnp.ones((col_count,), jnp.float32).at[masked_bins].set(0.0)
    kept_rows = lax.dynamic_slice_in_dim(kept_bins, first_bin + first_row, rows_here)
    kept_total = jnp.float32(col_count - masked_bins.shape[0])
    zscores = normalize(smoothed, expected_map, kept_rows, kept_bins, kept_total)
    return gram_rows(zscores, "blk") / kept_total


def solution(mesh):
    return jax.shard_map(
        shards,
        mesh=mesh,
        in_specs=(P(("groups", "blk"), None), P("groups"), P("groups"), P("groups")),
        out_specs=P(("groups", "blk"), None),
        check_vma=False,
    )
```

```python
import jax
import jax.numpy as jnp
from jax import lax
from jax.sharding import PartitionSpec as P

WMAX = 3


def with_halo(cells, sides, width):
    for axis, dim in sides:
        count = lax.axis_size(axis)
        ends = count - 1
        head = lax.slice_in_dim(cells, 0, width, axis=dim)
        tail = lax.slice_in_dim(cells, cells.shape[dim] - width, cells.shape[dim], axis=dim)
        cells = jnp.concatenate(
            [
                lax.ppermute(tail, axis, [(i, (i + 1) % count) for i in range(ends)]),
                cells,
                lax.ppermute(head, axis, [((i + 1) % count, i) for i in range(ends)]),
            ],
            axis=dim,
        )
    return cells


def smooth(padded, radius_map):
    rows_here = padded.shape[0] - 2 * WMAX
    col_count = padded.shape[1] - 2 * WMAX
    row_sums = padded[WMAX : WMAX + rows_here]
    smoothed = jnp.zeros((rows_here, col_count), jnp.float32)
    for radius in range(WMAX + 1):
        if radius > 0:
            row_sums = (
                row_sums
                + padded[WMAX - radius : WMAX - radius + rows_here]
                + padded[WMAX + radius : WMAX + radius + rows_here]
            )
        box_sums = row_sums[:, WMAX : WMAX + col_count]
        for offset in range(1, radius + 1):
            box_sums = (
                box_sums
                + row_sums[:, WMAX - offset : WMAX - offset + col_count]
                + row_sums[:, WMAX + offset : WMAX + offset + col_count]
            )
        smoothed = smoothed + jnp.where(
            radius_map == radius, box_sums / float((2 * radius + 1) ** 2), 0.0
        )
    return smoothed


def pair_counts(first_bin, nrows, col_count):
    distance = jnp.arange(col_count, dtype=jnp.int32)
    upper_pairs = jnp.clip(col_count - distance - first_bin, 0, nrows)
    lower_pairs = jnp.clip(first_bin + nrows - distance, 0, nrows)
    pair_total = jnp.where(distance == 0, nrows, upper_pairs + lower_pairs)
    return jnp.maximum(pair_total, 1).astype(jnp.float32)


def mirrored_table(table, margin=0):
    mirrored = jnp.concatenate([table[1:][::-1], table])
    return jnp.pad(mirrored, margin, mode="edge")


def skewed_map(table, window_first, rows_here, col_count, margin=0):
    span = col_count + rows_here - 1
    window = lax.dynamic_slice_in_dim(
        mirrored_table(table, margin), window_first + margin, span
    )
    tiled = jnp.tile(window, rows_here + 1)
    flat = tiled[rows_here - 1 : rows_here - 1 + rows_here * (span - 1)]
    return flat.reshape(rows_here, span - 1)[:, :col_count]


def diagonal_totals(smoothed, window_first, margin=0):
    rows_here = smoothed.shape[0]
    col_count = smoothed.shape[1]
    span = col_count + rows_here - 1
    placed = jnp.pad(smoothed, ((0, 0), (rows_here - 1, 0)))
    flat = jnp.pad(placed.reshape(rows_here * span), (0, rows_here))
    offsets = jnp.sum(flat.reshape(rows_here, span + 1), axis=0)[:span]
    spread = lax.dynamic_update_slice_in_dim(
        jnp.zeros((2 * col_count - 1 + 2 * margin,), jnp.float32),
        offsets,
        window_first + margin,
        0,
    )[margin : margin + 2 * col_count - 1]
    lower = jnp.concatenate([jnp.zeros((1,), jnp.float32), spread[: col_count - 1][::-1]])
    return spread[col_count - 1 :] + lower


def normalize(smoothed, expected_map, kept_rows, kept_cols, kept_total):
    ratio = smoothed / expected_map
    row_mean = jnp.sum(ratio * kept_cols[None, :], axis=1, keepdims=True) / kept_total
    centred = (ratio - row_mean) * kept_cols[None, :]
    variance = jnp.sum(centred * centred, axis=1, keepdims=True) / kept_total
    return (centred * lax.rsqrt(variance + 1e-05) * kept_rows[:, None]).astype(jnp.bfloat16)


def cross_block(left, right):
    return lax.dot_general(
        left, right, (((1,), (1,)), ((), ())), preferred_element_type=jnp.float32
    )


def tree_sum(values, axis):
    count = lax.axis_size(axis)
    if count & (count - 1):
        return lax.psum(values, axis)
    step = 1
    while step < count:
        values = values + lax.ppermute(values, axis, [(i, i ^ step) for i in range(count)])
        step *= 2
    return values


def gram_rows(zscores, axis):
    blocks = lax.axis_size(axis)
    rows_here = zscores.shape[0]
    columns = lax.all_to_all(zscores, axis, 1, 0, tiled=True)
    partial = cross_block(columns, columns)
    pieces = lax.all_to_all(partial, axis, 0, 0, tiled=True)
    return jnp.sum(pieces.reshape(blocks, rows_here, pieces.shape[1]), axis=0)


def shards(contacts, widths, masked_bins, row_start):
    blocks = lax.axis_size("blk")
    position = lax.axis_index("blk")
    rows_here = contacts.shape[0]
    col_count = contacts.shape[1]
    nbins = rows_here * blocks
    first_row = position * rows_here
    first_bin = row_start[0]
    window_first = col_count - 1 - (first_bin + first_row + rows_here - 1)
    wide_rows = rows_here + 2 * WMAX
    wide_first = window_first - WMAX
    wide_radius = skewed_map(widths, wide_first, wide_rows, col_count, WMAX)
    own = jnp.pad(contacts, ((2 * WMAX, 2 * WMAX), (WMAX, WMAX)))
    target = first_row - WMAX + jnp.arange(wide_rows, dtype=jnp.int32)
    inside = (target >= 0) & (target < nbins)
    own_part = jnp.where(inside[:, None], smooth(own, wide_radius), 0.0)
    local_total = diagonal_totals(own_part, wide_first, WMAX)
    local_total, later = lax.optimization_barrier((local_total, contacts))
    radius_map = skewed_map(widths, window_first, rows_here, col_count)
    padded_rows = with_halo(later, (("blk", 0),), WMAX)
    padded = jnp.pad(padded_rows, ((0, 0), (WMAX, WMAX)))
    smoothed = smooth(padded, radius_map)
    denominator = pair_counts(first_bin, nbins, col_count)
    expected = tree_sum(local_total, "blk") / denominator
    expected_map = skewed_map(expected, window_first, rows_here, col_count)
    kept_bins = jnp.ones((col_count,), jnp.float32).at[masked_bins].set(0.0)
    kept_rows = lax.dynamic_slice_in_dim(kept_bins, first_bin + first_row, rows_here)
    kept_total = jnp.float32(col_count - masked_bins.shape[0])
    zscores = normalize(smoothed, expected_map, kept_rows, kept_bins, kept_total)
    return gram_rows(zscores, "blk") / kept_total


def solution(mesh):
    return jax.shard_map(
        shards,
        mesh=mesh,
        in_specs=(P(("groups", "blk"), None), P("groups"), P("groups"), P("groups")),
        out_specs=P(("groups", "blk"), None),
        check_vma=False,
    )
```

```python
import jax
import jax.numpy as jnp
from jax import lax
from jax.sharding import PartitionSpec as P

WMAX = 3


def with_halo(cells, sides, width):
    for axis, dim in sides:
        count = lax.axis_size(axis)
        ends = count - 1
        head = lax.slice_in_dim(cells, 0, width, axis=dim)
        tail = lax.slice_in_dim(cells, cells.shape[dim] - width, cells.shape[dim], axis=dim)
        cells = jnp.concatenate(
            [
                lax.ppermute(tail, axis, [(i, (i + 1) % count) for i in range(ends)]),
                cells,
                lax.ppermute(head, axis, [((i + 1) % count, i) for i in range(ends)]),
            ],
            axis=dim,
        )
    return cells


def smooth(padded, radius_map):
    rows_here = padded.shape[0] - 2 * WMAX
    col_count = padded.shape[1] - 2 * WMAX
    row_sums = padded[WMAX : WMAX + rows_here]
    smoothed = jnp.zeros((rows_here, col_count), jnp.float32)
    for radius in range(WMAX + 1):
        if radius > 0:
            row_sums = (
                row_sums
                + padded[WMAX - radius : WMAX - radius + rows_here]
                + padded[WMAX + radius : WMAX + radius + rows_here]
            )
        box_sums = row_sums[:, WMAX : WMAX + col_count]
        for offset in range(1, radius + 1):
            box_sums = (
                box_sums
                + row_sums[:, WMAX - offset : WMAX - offset + col_count]
                + row_sums[:, WMAX + offset : WMAX + offset + col_count]
            )
        smoothed = smoothed + jnp.where(
            radius_map == radius, box_sums / float((2 * radius + 1) ** 2), 0.0
        )
    return smoothed


def pair_counts(first_bin, nrows, col_count):
    distance = jnp.arange(col_count, dtype=jnp.int32)
    upper_pairs = jnp.clip(col_count - distance - first_bin, 0, nrows)
    lower_pairs = jnp.clip(first_bin + nrows - distance, 0, nrows)
    pair_total = jnp.where(distance == 0, nrows, upper_pairs + lower_pairs)
    return jnp.maximum(pair_total, 1).astype(jnp.float32)


def mirrored_table(table):
    return jnp.concatenate([table[1:][::-1], table])


def skewed_map(table, window_first, rows_here, col_count):
    span = col_count + rows_here - 1
    window = lax.dynamic_slice_in_dim(mirrored_table(table), window_first, span)
    tiled = jnp.tile(window, rows_here + 1)
    flat = tiled[rows_here - 1 : rows_here - 1 + rows_here * (span - 1)]
    return flat.reshape(rows_here, span - 1)[:, :col_count]


def diagonal_totals(smoothed, window_first):
    rows_here = smoothed.shape[0]
    col_count = smoothed.shape[1]
    span = col_count + rows_here - 1
    placed = jnp.pad(smoothed, ((0, 0), (rows_here - 1, 0)))
    flat = jnp.pad(placed.reshape(rows_here * span), (0, rows_here))
    offsets = jnp.sum(flat.reshape(rows_here, span + 1), axis=0)[:span]
    spread = lax.dynamic_update_slice_in_dim(
        jnp.zeros((2 * col_count - 1,), jnp.float32), offsets, window_first, 0
    )
    lower = jnp.concatenate([jnp.zeros((1,), jnp.float32), spread[: col_count - 1][::-1]])
    return spread[col_count - 1 :] + lower


def normalize(smoothed, expected_map, kept_rows, kept_cols, kept_total):
    ratio = smoothed / expected_map
    row_mean = jnp.sum(ratio * kept_cols[None, :], axis=1, keepdims=True) / kept_total
    centred = (ratio - row_mean) * kept_cols[None, :]
    variance = jnp.sum(centred * centred, axis=1, keepdims=True) / kept_total
    return (centred * lax.rsqrt(variance + 1e-05) * kept_rows[:, None]).astype(jnp.bfloat16)


def cross_block(left, right):
    return lax.dot_general(
        left, right, (((1,), (1,)), ((), ())), preferred_element_type=jnp.float32
    )


def tree_sum(values, axis):
    count = lax.axis_size(axis)
    if count & (count - 1):
        return lax.psum(values, axis)
    step = 1
    while step < count:
        values = values + lax.ppermute(values, axis, [(i, i ^ step) for i in range(count)])
        step *= 2
    return values


def gram_rows(zscores, axis):
    blocks = lax.axis_size(axis)
    rows_here = zscores.shape[0]
    columns = lax.all_to_all(zscores, axis, 1, 0, tiled=True)
    partial = cross_block(columns, columns)
    pieces = lax.all_to_all(partial, axis, 0, 0, tiled=True)
    return jnp.sum(pieces.reshape(blocks, rows_here, pieces.shape[1]), axis=0)


def shards(contacts, widths, masked_bins, row_start):
    blocks = lax.axis_size("blk")
    position = lax.axis_index("blk")
    rows_here = contacts.shape[0]
    col_count = contacts.shape[1]
    nbins = rows_here * blocks
    first_row = position * rows_here
    first_bin = row_start[0]
    window_first = col_count - 1 - (first_bin + first_row + rows_here - 1)
    radius_map = skewed_map(widths, window_first, rows_here, col_count)
    kept_bins = jnp.ones((col_count,), jnp.float32).at[masked_bins].set(0.0)
    padded_rows, kept_bins = lax.optimization_barrier(
        (with_halo(contacts, (("blk", 0),), WMAX), kept_bins)
    )
    padded = jnp.pad(padded_rows, ((0, 0), (WMAX, WMAX)))
    smoothed = smooth(padded, radius_map)
    local_total = diagonal_totals(smoothed, window_first)
    denominator = pair_counts(first_bin, nbins, col_count)
    expected = tree_sum(local_total, "blk") / denominator
    expected_map = skewed_map(expected, window_first, rows_here, col_count)
    kept_rows = lax.dynamic_slice_in_dim(kept_bins, first_bin + first_row, rows_here)
    kept_total = jnp.float32(col_count - masked_bins.shape[0])
    zscores = normalize(smoothed, expected_map, kept_rows, kept_bins, kept_total)
    return gram_rows(zscores, "blk") / kept_total


def solution(mesh):
    return jax.shard_map(
        shards,
        mesh=mesh,
        in_specs=(P(("groups", "blk"), None), P("groups"), P("groups"), P("groups")),
        out_specs=P(("groups", "blk"), None),
        check_vma=False,
    )
```

```python
import jax
import jax.numpy as jnp
from jax import lax
from jax.sharding import PartitionSpec as P

WMAX = 3


def with_halo(cells, sides, width):
    for axis, dim in sides:
        count = lax.axis_size(axis)
        head = lax.slice_in_dim(cells, 0, width, axis=dim)
        tail = lax.slice_in_dim(cells, cells.shape[dim] - width, cells.shape[dim], axis=dim)
        if count % 2:
            ends = count - 1
            before = lax.ppermute(tail, axis, [(i, (i + 1) % count) for i in range(ends)])
            after = lax.ppermute(head, axis, [((i + 1) % count, i) for i in range(ends)])
        else:
            odd = lax.axis_index(axis) % 2 == 1
            inner = lax.ppermute(
                jnp.where(odd, head, tail), axis, [(i, i ^ 1) for i in range(count)]
            )
            outer = lax.ppermute(
                jnp.where(odd, tail, head),
                axis,
                [(i, i - 1) for i in range(2, count, 2)]
                + [(i, i + 1) for i in range(1, count - 1, 2)],
            )
            before = jnp.where(odd, inner, outer)
            after = jnp.where(odd, outer, inner)
        cells = jnp.concatenate([before, cells, after], axis=dim)
    return cells


def smooth(padded, radius_map):
    rows_here = padded.shape[0] - 2 * WMAX
    col_count = padded.shape[1] - 2 * WMAX
    row_sums = padded[WMAX : WMAX + rows_here]
    smoothed = jnp.zeros((rows_here, col_count), jnp.float32)
    for radius in range(WMAX + 1):
        if radius > 0:
            row_sums = (
                row_sums
                + padded[WMAX - radius : WMAX - radius + rows_here]
                + padded[WMAX + radius : WMAX + radius + rows_here]
            )
        box_sums = row_sums[:, WMAX : WMAX + col_count]
        for offset in range(1, radius + 1):
            box_sums = (
                box_sums
                + row_sums[:, WMAX - offset : WMAX - offset + col_count]
                + row_sums[:, WMAX + offset : WMAX + offset + col_count]
            )
        smoothed = smoothed + jnp.where(
            radius_map == radius, box_sums / float((2 * radius + 1) ** 2), 0.0
        )
    return smoothed


def pair_counts(first_bin, nrows, col_count):
    distance = jnp.arange(col_count, dtype=jnp.int32)
    upper_pairs = jnp.clip(col_count - distance - first_bin, 0, nrows)
    lower_pairs = jnp.clip(first_bin + nrows - distance, 0, nrows)
    pair_total = jnp.where(distance == 0, nrows, upper_pairs + lower_pairs)
    return jnp.maximum(pair_total, 1).astype(jnp.float32)


def mirrored_table(table):
    return jnp.concatenate([table[1:][::-1], table])


def skewed_map(table, window_first, rows_here, col_count):
    span = col_count + rows_here - 1
    window = lax.dynamic_slice_in_dim(mirrored_table(table), window_first, span)
    tiled = jnp.tile(window, rows_here + 1)
    flat = tiled[rows_here - 1 : rows_here - 1 + rows_here * (span - 1)]
    return flat.reshape(rows_here, span - 1)[:, :col_count]


def diagonal_totals(smoothed, window_first):
    rows_here = smoothed.shape[0]
    col_count = smoothed.shape[1]
    span = col_count + rows_here - 1
    placed = jnp.pad(smoothed, ((0, 0), (rows_here - 1, 0)))
    flat = jnp.pad(placed.reshape(rows_here * span), (0, rows_here))
    offsets = jnp.sum(flat.reshape(rows_here, span + 1), axis=0)[:span]
    spread = lax.dynamic_update_slice_in_dim(
        jnp.zeros((2 * col_count - 1,), jnp.float32), offsets, window_first, 0
    )
    lower = jnp.concatenate([jnp.zeros((1,), jnp.float32), spread[: col_count - 1][::-1]])
    return spread[col_count - 1 :] + lower


def normalize(smoothed, expected_map, kept_rows, kept_cols, kept_total):
    ratio = smoothed / expected_map
    row_mean = jnp.sum(ratio * kept_cols[None, :], axis=1, keepdims=True) / kept_total
    centred = (ratio - row_mean) * kept_cols[None, :]
    variance = jnp.sum(centred * centred, axis=1, keepdims=True) / kept_total
    return (centred * lax.rsqrt(variance + 1e-05) * kept_rows[:, None]).astype(jnp.bfloat16)


def cross_block(left, right):
    return lax.dot_general(
        left, right, (((1,), (1,)), ((), ())), preferred_element_type=jnp.float32
    )


def tree_sum(values, axis):
    count = lax.axis_size(axis)
    if count & (count - 1):
        return lax.psum(values, axis)
    step = 1
    while step < count:
        values = values + lax.ppermute(values, axis, [(i, i ^ step) for i in range(count)])
        step *= 2
    return values


def gram_rows(zscores, axis):
    blocks = lax.axis_size(axis)
    rows_here = zscores.shape[0]
    columns = lax.all_to_all(zscores, axis, 1, 0, tiled=True)
    partial = cross_block(columns, columns)
    pieces = lax.all_to_all(partial, axis, 0, 0, tiled=True)
    return jnp.sum(pieces.reshape(blocks, rows_here, pieces.shape[1]), axis=0)


def shards(contacts, widths, masked_bins, row_start):
    blocks = lax.axis_size("blk")
    position = lax.axis_index("blk")
    rows_here = contacts.shape[0]
    col_count = contacts.shape[1]
    nbins = rows_here * blocks
    first_row = position * rows_here
    first_bin = row_start[0]
    window_first = col_count - 1 - (first_bin + first_row + rows_here - 1)
    radius_map = skewed_map(widths, window_first, rows_here, col_count)
    padded_rows = with_halo(contacts, (("blk", 0),), WMAX)
    padded = jnp.pad(padded_rows, ((0, 0), (WMAX, WMAX)))
    smoothed = smooth(padded, radius_map)
    local_total = diagonal_totals(smoothed, window_first)
    denominator = pair_counts(first_bin, nbins, col_count)
    expected = tree_sum(local_total, "blk") / denominator
    expected_map = skewed_map(expected, window_first, rows_here, col_count)
    kept_bins = jnp.ones((col_count,), jnp.float32).at[masked_bins].set(0.0)
    kept_rows = lax.dynamic_slice_in_dim(kept_bins, first_bin + first_row, rows_here)
    kept_total = jnp.float32(col_count - masked_bins.shape[0])
    zscores = normalize(smoothed, expected_map, kept_rows, kept_bins, kept_total)
    return gram_rows(zscores, "blk") / kept_total


def solution(mesh):
    return jax.shard_map(
        shards,
        mesh=mesh,
        in_specs=(P(("groups", "blk"), None), P("groups"), P("groups"), P("groups")),
        out_specs=P(("groups", "blk"), None),
        check_vma=False,
    )
```

```python
import jax
import jax.numpy as jnp
from jax import lax
from jax.sharding import PartitionSpec as P

WMAX = 3


def with_halo(cells, sides, width):
    for axis, dim in sides:
        count = lax.axis_size(axis)
        head = lax.slice_in_dim(cells, 0, width, axis=dim)
        tail = lax.slice_in_dim(cells, cells.shape[dim] - width, cells.shape[dim], axis=dim)
        if count % 2:
            ends = count - 1
            before = lax.ppermute(tail, axis, [(i, (i + 1) % count) for i in range(ends)])
            after = lax.ppermute(head, axis, [((i + 1) % count, i) for i in range(ends)])
        else:
            odd = lax.axis_index(axis) % 2 == 1
            inner = lax.ppermute(
                jnp.where(odd, head, tail), axis, [(i, i ^ 1) for i in range(count)]
            )
            outer = lax.ppermute(
                jnp.where(odd, tail, head),
                axis,
                [(i, i - 1) for i in range(2, count, 2)]
                + [(i, i + 1) for i in range(1, count - 1, 2)],
            )
            before = jnp.where(odd, inner, outer)
            after = jnp.where(odd, outer, inner)
        cells = jnp.concatenate([before, cells, after], axis=dim)
    return cells


def smooth(padded, radius_map):
    rows_here = padded.shape[0] - 2 * WMAX
    col_count = padded.shape[1] - 2 * WMAX
    row_sums = padded[WMAX : WMAX + rows_here]
    smoothed = jnp.zeros((rows_here, col_count), jnp.float32)
    for radius in range(WMAX + 1):
        if radius > 0:
            row_sums = (
                row_sums
                + padded[WMAX - radius : WMAX - radius + rows_here]
                + padded[WMAX + radius : WMAX + radius + rows_here]
            )
        box_sums = row_sums[:, WMAX : WMAX + col_count]
        for offset in range(1, radius + 1):
            box_sums = (
                box_sums
                + row_sums[:, WMAX - offset : WMAX - offset + col_count]
                + row_sums[:, WMAX + offset : WMAX + offset + col_count]
            )
        smoothed = smoothed + jnp.where(
            radius_map == radius, box_sums / float((2 * radius + 1) ** 2), 0.0
        )
    return smoothed


def pair_counts(first_bin, nrows, col_count):
    distance = jnp.arange(col_count, dtype=jnp.int32)
    upper_pairs = jnp.clip(col_count - distance - first_bin, 0, nrows)
    lower_pairs = jnp.clip(first_bin + nrows - distance, 0, nrows)
    pair_total = jnp.where(distance == 0, nrows, upper_pairs + lower_pairs)
    return jnp.maximum(pair_total, 1).astype(jnp.float32)


def mirrored_table(table):
    return jnp.concatenate([table[1:][::-1], table])


def skewed_map(table, window_first, rows_here, col_count):
    span = col_count + rows_here - 1
    window = lax.dynamic_slice_in_dim(mirrored_table(table), window_first, span)
    tiled = jnp.tile(window, rows_here + 1)
    flat = tiled[rows_here - 1 : rows_here - 1 + rows_here * (span - 1)]
    return flat.reshape(rows_here, span - 1)[:, :col_count]


def diagonal_totals(smoothed, window_first):
    rows_here = smoothed.shape[0]
    col_count = smoothed.shape[1]
    span = col_count + rows_here - 1
    placed = jnp.pad(smoothed, ((0, 0), (rows_here - 1, 0)))
    flat = jnp.pad(placed.reshape(rows_here * span), (0, rows_here))
    offsets = jnp.sum(flat.reshape(rows_here, span + 1), axis=0)[:span]
    spread = lax.dynamic_update_slice_in_dim(
        jnp.zeros((2 * col_count - 1,), jnp.float32), offsets, window_first, 0
    )
    lower = jnp.concatenate([jnp.zeros((1,), jnp.float32), spread[: col_count - 1][::-1]])
    return spread[col_count - 1 :] + lower


def normalize(smoothed, expected_map, kept_rows, kept_cols, kept_total):
    ratio = smoothed / expected_map
    row_mean = jnp.sum(ratio * kept_cols[None, :], axis=1, keepdims=True) / kept_total
    centred = (ratio - row_mean) * kept_cols[None, :]
    variance = jnp.sum(centred * centred, axis=1, keepdims=True) / kept_total
    return (centred * lax.rsqrt(variance + 1e-05) * kept_rows[:, None]).astype(jnp.bfloat16)


def cross_block(left, right):
    return lax.dot_general(
        left, right, (((1,), (1,)), ((), ())), preferred_element_type=jnp.float32
    )


def tree_sum(values, axis):
    count = lax.axis_size(axis)
    if count & (count - 1):
        return lax.psum(values, axis)
    step = count // 2
    while step:
        values = values + lax.ppermute(values, axis, [(i, i ^ step) for i in range(count)])
        step //= 2
    return values


def gram_rows(zscores, axis):
    blocks = lax.axis_size(axis)
    rows_here = zscores.shape[0]
    columns = lax.all_to_all(zscores, axis, 1, 0, tiled=True)
    partial = cross_block(columns, columns)
    pieces = lax.all_to_all(partial, axis, 0, 0, tiled=True)
    return jnp.sum(pieces.reshape(blocks, rows_here, pieces.shape[1]), axis=0)


def shards(contacts, widths, masked_bins, row_start):
    blocks = lax.axis_size("blk")
    position = lax.axis_index("blk")
    rows_here = contacts.shape[0]
    col_count = contacts.shape[1]
    nbins = rows_here * blocks
    first_row = position * rows_here
    first_bin = row_start[0]
    window_first = col_count - 1 - (first_bin + first_row + rows_here - 1)
    radius_map = skewed_map(widths, window_first, rows_here, col_count)
    padded_rows = with_halo(contacts, (("blk", 0),), WMAX)
    padded = jnp.pad(padded_rows, ((0, 0), (WMAX, WMAX)))
    smoothed = smooth(padded, radius_map)
    local_total = diagonal_totals(smoothed, window_first)
    denominator = pair_counts(first_bin, nbins, col_count)
    expected = tree_sum(local_total, "blk") / denominator
    expected_map = skewed_map(expected, window_first, rows_here, col_count)
    kept_bins = jnp.ones((col_count,), jnp.float32).at[masked_bins].set(0.0)
    kept_rows = lax.dynamic_slice_in_dim(kept_bins, first_bin + first_row, rows_here)
    kept_total = jnp.float32(col_count - masked_bins.shape[0])
    zscores = normalize(smoothed, expected_map, kept_rows, kept_bins, kept_total)
    return gram_rows(zscores, "blk") / kept_total


def solution(mesh):
    return jax.shard_map(
        shards,
        mesh=mesh,
        in_specs=(P(("groups", "blk"), None), P("groups"), P("groups"), P("groups")),
        out_specs=P(("groups", "blk"), None),
        check_vma=False,
    )
```

```python
import jax
import jax.numpy as jnp
from jax import lax
from jax.sharding import PartitionSpec as P

WMAX = 3


def with_halo(cells, sides, width):
    for axis, dim in sides:
        count = lax.axis_size(axis)
        head = lax.slice_in_dim(cells, 0, width, axis=dim)
        tail = lax.slice_in_dim(cells, cells.shape[dim] - width, cells.shape[dim], axis=dim)
        if count % 2:
            ends = count - 1
            before = lax.ppermute(tail, axis, [(i, (i + 1) % count) for i in range(ends)])
            after = lax.ppermute(head, axis, [((i + 1) % count, i) for i in range(ends)])
        else:
            odd = lax.axis_index(axis) % 2 == 1
            inner = lax.ppermute(
                jnp.where(odd, head, tail), axis, [(i, i ^ 1) for i in range(count)]
            )
            outer = lax.ppermute(
                jnp.where(odd, tail, head),
                axis,
                [(i, i - 1) for i in range(2, count, 2)]
                + [(i, i + 1) for i in range(1, count - 1, 2)],
            )
            before = jnp.where(odd, inner, outer)
            after = jnp.where(odd, outer, inner)
        cells = jnp.concatenate([before, cells, after], axis=dim)
    return cells


def smooth(padded, radius_map):
    rows_here = padded.shape[0] - 2 * WMAX
    col_count = padded.shape[1] - 2 * WMAX
    row_sums = padded[WMAX : WMAX + rows_here]
    smoothed = jnp.zeros((rows_here, col_count), jnp.float32)
    for radius in range(WMAX + 1):
        if radius > 0:
            row_sums = (
                row_sums
                + padded[WMAX - radius : WMAX - radius + rows_here]
                + padded[WMAX + radius : WMAX + radius + rows_here]
            )
        box_sums = row_sums[:, WMAX : WMAX + col_count]
        for offset in range(1, radius + 1):
            box_sums = (
                box_sums
                + row_sums[:, WMAX - offset : WMAX - offset + col_count]
                + row_sums[:, WMAX + offset : WMAX + offset + col_count]
            )
        smoothed = smoothed + jnp.where(
            radius_map == radius, box_sums / float((2 * radius + 1) ** 2), 0.0
        )
    return smoothed


def pair_counts(first_bin, nrows, col_count):
    distance = jnp.arange(col_count, dtype=jnp.int32)
    upper_pairs = jnp.clip(col_count - distance - first_bin, 0, nrows)
    lower_pairs = jnp.clip(first_bin + nrows - distance, 0, nrows)
    pair_total = jnp.where(distance == 0, nrows, upper_pairs + lower_pairs)
    return jnp.maximum(pair_total, 1).astype(jnp.float32)


def mirrored_table(table):
    return jnp.concatenate([table[1:][::-1], table])


def skewed_map(table, window_first, rows_here, col_count):
    span = col_count + rows_here - 1
    window = lax.dynamic_slice_in_dim(mirrored_table(table), window_first, span)
    tiled = jnp.tile(window, rows_here + 1)
    flat = tiled[rows_here - 1 : rows_here - 1 + rows_here * (span - 1)]
    return flat.reshape(rows_here, span - 1)[:, :col_count]


def diagonal_totals(smoothed, window_first):
    rows_here = smoothed.shape[0]
    col_count = smoothed.shape[1]
    span = col_count + rows_here - 1
    placed = jnp.pad(smoothed, ((0, 0), (rows_here - 1, 0)))
    flat = jnp.pad(placed.reshape(rows_here * span), (0, rows_here))
    offsets = jnp.sum(flat.reshape(rows_here, span + 1), axis=0)[:span]
    spread = lax.dynamic_update_slice_in_dim(
        jnp.zeros((2 * col_count - 1,), jnp.float32), offsets, window_first, 0
    )
    lower = jnp.concatenate([jnp.zeros((1,), jnp.float32), spread[: col_count - 1][::-1]])
    return spread[col_count - 1 :] + lower


def normalize(smoothed, expected_map, kept_rows, kept_cols, kept_total):
    ratio = smoothed / expected_map
    row_mean = jnp.sum(ratio * kept_cols[None, :], axis=1, keepdims=True) / kept_total
    centred = (ratio - row_mean) * kept_cols[None, :]
    variance = jnp.sum(centred * centred, axis=1, keepdims=True) / kept_total
    return (centred * lax.rsqrt(variance + 1e-05) * kept_rows[:, None]).astype(jnp.bfloat16)


def cross_block(left, right):
    return lax.dot_general(
        left, right, (((1,), (1,)), ((), ())), preferred_element_type=jnp.float32
    )


def tree_sum(values, axis):
    count = lax.axis_size(axis)
    if count & (count - 1):
        return lax.psum(values, axis)
    step = 1
    while step < count:
        values = values + lax.ppermute(values, axis, [(i, i ^ step) for i in range(count)])
        step *= 2
    return values


def gram_rows(zscores, axis):
    blocks = lax.axis_size(axis)
    rows_here = zscores.shape[0]
    columns = lax.all_to_all(zscores, axis, 1, 0, tiled=True)
    partial = cross_block(columns, columns)
    pieces = lax.all_to_all(partial, axis, 0, 0, tiled=True)
    return jnp.sum(pieces.reshape(blocks, rows_here, pieces.shape[1]), axis=0)


def shards(contacts, widths, masked_bins, row_start):
    blocks = lax.axis_size("blk")
    position = lax.axis_index("blk")
    rows_here = contacts.shape[0]
    col_count = contacts.shape[1]
    nbins = rows_here * blocks
    first_row = position * rows_here
    first_bin = row_start[0]
    window_first = col_count - 1 - (first_bin + first_row + rows_here - 1)
    radius_map = skewed_map(widths, window_first, rows_here, col_count)
    own = lax.optimization_barrier(jnp.pad(contacts, WMAX))
    halo = with_halo(contacts, (("blk", 0),), WMAX)
    padded = own.at[:WMAX, WMAX:-WMAX].set(halo[:WMAX]).at[-WMAX:, WMAX:-WMAX].set(halo[-WMAX:])
    smoothed = smooth(padded, radius_map)
    local_total = diagonal_totals(smoothed, window_first)
    denominator = pair_counts(first_bin, nbins, col_count)
    expected = tree_sum(local_total, "blk") / denominator
    expected_map = skewed_map(expected, window_first, rows_here, col_count)
    kept_bins = jnp.ones((col_count,), jnp.float32).at[masked_bins].set(0.0, unique_indices=True)
    kept_rows = lax.dynamic_slice_in_dim(kept_bins, first_bin + first_row, rows_here)
    kept_total = jnp.float32(col_count - masked_bins.shape[0])
    zscores = normalize(smoothed, expected_map, kept_rows, kept_bins, kept_total)
    return gram_rows(zscores, "blk") / kept_total


def solution(mesh):
    return jax.shard_map(
        shards,
        mesh=mesh,
        in_specs=(P(("groups", "blk"), None), P("groups"), P("groups"), P("groups")),
        out_specs=P(("groups", "blk"), None),
        check_vma=False,
    )
```

```python
import jax
import jax.numpy as jnp
from jax import lax
from jax.sharding import PartitionSpec as P

WMAX = 3


def with_halo(cells, sides, width):
    for axis, dim in sides:
        count = lax.axis_size(axis)
        head = lax.slice_in_dim(cells, 0, width, axis=dim)
        tail = lax.slice_in_dim(cells, cells.shape[dim] - width, cells.shape[dim], axis=dim)
        if count % 2:
            ends = count - 1
            before = lax.ppermute(tail, axis, [(i, (i + 1) % count) for i in range(ends)])
            after = lax.ppermute(head, axis, [((i + 1) % count, i) for i in range(ends)])
        else:
            odd = lax.axis_index(axis) % 2 == 1
            inner = lax.ppermute(
                jnp.where(odd, head, tail), axis, [(i, i ^ 1) for i in range(count)]
            )
            outer = lax.ppermute(
                jnp.where(odd, tail, head),
                axis,
                [(i, i - 1) for i in range(2, count, 2)]
                + [(i, i + 1) for i in range(1, count - 1, 2)],
            )
            before = jnp.where(odd, inner, outer)
            after = jnp.where(odd, outer, inner)
        cells = jnp.concatenate([before, cells, after], axis=dim)
    return cells


def smooth(padded, radius_map):
    rows_here = padded.shape[0] - 2 * WMAX
    col_count = padded.shape[1] - 2 * WMAX
    row_sums = padded[WMAX : WMAX + rows_here]
    smoothed = jnp.zeros((rows_here, col_count), jnp.float32)
    for radius in range(WMAX + 1):
        if radius > 0:
            row_sums = (
                row_sums
                + padded[WMAX - radius : WMAX - radius + rows_here]
                + padded[WMAX + radius : WMAX + radius + rows_here]
            )
        box_sums = row_sums[:, WMAX : WMAX + col_count]
        for offset in range(1, radius + 1):
            box_sums = (
                box_sums
                + row_sums[:, WMAX - offset : WMAX - offset + col_count]
                + row_sums[:, WMAX + offset : WMAX + offset + col_count]
            )
        smoothed = smoothed + jnp.where(
            radius_map == radius, box_sums / float((2 * radius + 1) ** 2), 0.0
        )
    return smoothed


def pair_counts(first_bin, nrows, col_count):
    distance = jnp.arange(col_count, dtype=jnp.int32)
    upper_pairs = jnp.clip(col_count - distance - first_bin, 0, nrows)
    lower_pairs = jnp.clip(first_bin + nrows - distance, 0, nrows)
    pair_total = jnp.where(distance == 0, nrows, upper_pairs + lower_pairs)
    return jnp.maximum(pair_total, 1).astype(jnp.float32)


def mirrored_table(table):
    return jnp.concatenate([table[1:][::-1], table])


def skewed_map(table, window_first, rows_here, col_count):
    span = col_count + rows_here - 1
    window = lax.dynamic_slice_in_dim(mirrored_table(table), window_first, span)
    tiled = jnp.tile(window, rows_here + 1)
    flat = tiled[rows_here - 1 : rows_here - 1 + rows_here * (span - 1)]
    return flat.reshape(rows_here, span - 1)[:, :col_count]


def diagonal_totals(smoothed, window_first):
    rows_here = smoothed.shape[0]
    col_count = smoothed.shape[1]
    span = col_count + rows_here - 1
    placed = jnp.pad(smoothed, ((0, 0), (rows_here - 1, 0)))
    flat = jnp.pad(placed.reshape(rows_here * span), (0, rows_here))
    offsets = jnp.sum(flat.reshape(rows_here, span + 1), axis=0)[:span]
    spread = lax.dynamic_update_slice_in_dim(
        jnp.zeros((2 * col_count - 1,), jnp.float32), offsets, window_first, 0
    )
    lower = jnp.concatenate([jnp.zeros((1,), jnp.float32), spread[: col_count - 1][::-1]])
    return spread[col_count - 1 :] + lower


def normalize(smoothed, expected_map, kept_rows, kept_cols, kept_total):
    ratio = smoothed / expected_map
    row_mean = jnp.sum(ratio * kept_cols[None, :], axis=1, keepdims=True) / kept_total
    centred = (ratio - row_mean) * kept_cols[None, :]
    variance = jnp.sum(centred * centred, axis=1, keepdims=True) / kept_total
    return (centred * lax.rsqrt(variance + 1e-05) * kept_rows[:, None]).astype(jnp.bfloat16)


def cross_block(left, right):
    return lax.dot_general(
        left, right, (((1,), (1,)), ((), ())), preferred_element_type=jnp.float32
    )


def tree_sum(values, axis):
    count = lax.axis_size(axis)
    if count & (count - 1):
        return lax.psum(values, axis)
    step = 1
    while step < count:
        values = values + lax.ppermute(values, axis, [(i, i ^ step) for i in range(count)])
        step *= 2
    return values


def gram_rows(zscores, axis):
    blocks = lax.axis_size(axis)
    rows_here = zscores.shape[0]
    columns = lax.all_to_all(zscores, axis, 1, 0, tiled=True)
    partial = cross_block(columns, columns)
    pieces = lax.all_to_all(partial, axis, 0, 0, tiled=True)
    return jnp.sum(pieces.reshape(blocks, rows_here, pieces.shape[1]), axis=0)


def shards(contacts, widths, masked_bins, row_start):
    blocks = lax.axis_size("blk")
    position = lax.axis_index("blk")
    rows_here = contacts.shape[0]
    col_count = contacts.shape[1]
    nbins = rows_here * blocks
    first_row = position * rows_here
    first_bin = row_start[0]
    window_first = col_count - 1 - (first_bin + first_row + rows_here - 1)
    radius_map = skewed_map(widths, window_first, rows_here, col_count)
    own = lax.optimization_barrier(jnp.pad(contacts, WMAX))
    halo = with_halo(contacts, (("blk", 0),), WMAX)
    padded = lax.dynamic_update_slice(own, halo[:WMAX], (0, WMAX))
    padded = lax.dynamic_update_slice(padded, halo[-WMAX:], (rows_here + WMAX, WMAX))
    smoothed = smooth(padded, radius_map)
    local_total = diagonal_totals(smoothed, window_first)
    denominator = pair_counts(first_bin, nbins, col_count)
    expected = tree_sum(local_total, "blk") / denominator
    expected_map = skewed_map(expected, window_first, rows_here, col_count)
    kept_bins = jnp.ones((col_count,), jnp.float32).at[masked_bins].set(0.0)
    kept_rows = lax.dynamic_slice_in_dim(kept_bins, first_bin + first_row, rows_here)
    kept_total = jnp.float32(col_count - masked_bins.shape[0])
    zscores = normalize(smoothed, expected_map, kept_rows, kept_bins, kept_total)
    return gram_rows(zscores, "blk") / kept_total


def solution(mesh):
    return jax.shard_map(
        shards,
        mesh=mesh,
        in_specs=(P(("groups", "blk"), None), P("groups"), P("groups"), P("groups")),
        out_specs=P(("groups", "blk"), None),
        check_vma=False,
    )
```

```python
import jax
import jax.numpy as jnp
from jax import lax
from jax.sharding import PartitionSpec as P

WMAX = 3


def with_halo(cells, sides, width):
    for axis, dim in sides:
        count = lax.axis_size(axis)
        head = lax.slice_in_dim(cells, 0, width, axis=dim)
        tail = lax.slice_in_dim(cells, cells.shape[dim] - width, cells.shape[dim], axis=dim)
        if count % 2:
            ends = count - 1
            before = lax.ppermute(tail, axis, [(i, (i + 1) % count) for i in range(ends)])
            after = lax.ppermute(head, axis, [((i + 1) % count, i) for i in range(ends)])
        else:
            odd = lax.axis_index(axis) % 2 == 1
            inner = lax.ppermute(
                jnp.where(odd, head, tail), axis, [(i, i ^ 1) for i in range(count)]
            )
            outer = lax.ppermute(
                jnp.where(odd, tail, head),
                axis,
                [(i, i - 1) for i in range(2, count, 2)]
                + [(i, i + 1) for i in range(1, count - 1, 2)],
            )
            before = jnp.where(odd, inner, outer)
            after = jnp.where(odd, outer, inner)
        cells = jnp.concatenate([before, cells, after], axis=dim)
    return cells


def smooth(padded, radius_map):
    rows_here = padded.shape[0] - 2 * WMAX
    col_count = padded.shape[1] - 2 * WMAX
    row_sums = padded[WMAX : WMAX + rows_here]
    smoothed = jnp.zeros((rows_here, col_count), jnp.float32)
    for radius in range(WMAX + 1):
        if radius > 0:
            row_sums = (
                row_sums
                + padded[WMAX - radius : WMAX - radius + rows_here]
                + padded[WMAX + radius : WMAX + radius + rows_here]
            )
        box_sums = row_sums[:, WMAX : WMAX + col_count]
        for offset in range(1, radius + 1):
            box_sums = (
                box_sums
                + row_sums[:, WMAX - offset : WMAX - offset + col_count]
                + row_sums[:, WMAX + offset : WMAX + offset + col_count]
            )
        smoothed = smoothed + jnp.where(
            radius_map == radius, box_sums / float((2 * radius + 1) ** 2), 0.0
        )
    return smoothed


def pair_counts(first_bin, nrows, col_count):
    distance = jnp.arange(col_count, dtype=jnp.int32)
    upper_pairs = jnp.clip(col_count - distance - first_bin, 0, nrows)
    lower_pairs = jnp.clip(first_bin + nrows - distance, 0, nrows)
    pair_total = jnp.where(distance == 0, nrows, upper_pairs + lower_pairs)
    return jnp.maximum(pair_total, 1).astype(jnp.float32)


def mirrored_table(table):
    return jnp.concatenate([table[1:][::-1], table])


def skewed_map(table, window_first, rows_here, col_count):
    span = col_count + rows_here - 1
    window = lax.dynamic_slice_in_dim(mirrored_table(table), window_first, span)
    tiled = jnp.tile(window, rows_here + 1)
    flat = tiled[rows_here - 1 : rows_here - 1 + rows_here * (span - 1)]
    return flat.reshape(rows_here, span - 1)[:, :col_count]


def diagonal_totals(smoothed, window_first):
    rows_here = smoothed.shape[0]
    col_count = smoothed.shape[1]
    span = col_count + rows_here - 1
    placed = jnp.pad(smoothed, ((0, 0), (rows_here - 1, 0)))
    flat = jnp.pad(placed.reshape(rows_here * span), (0, rows_here))
    offsets = jnp.sum(flat.reshape(rows_here, span + 1), axis=0)[:span]
    spread = lax.dynamic_update_slice_in_dim(
        jnp.zeros((2 * col_count - 1,), jnp.float32), offsets, window_first, 0
    )
    lower = jnp.concatenate([jnp.zeros((1,), jnp.float32), spread[: col_count - 1][::-1]])
    return spread[col_count - 1 :] + lower


def normalize(smoothed, expected_map, kept_rows, kept_cols, kept_total):
    ratio = smoothed / expected_map
    row_mean = jnp.sum(ratio * kept_cols[None, :], axis=1, keepdims=True) / kept_total
    centred = (ratio - row_mean) * kept_cols[None, :]
    variance = jnp.sum(centred * centred, axis=1, keepdims=True) / kept_total
    return (centred * lax.rsqrt(variance + 1e-05) * kept_rows[:, None]).astype(jnp.bfloat16)


def cross_block(left, right):
    return lax.dot_general(
        left, right, (((1,), (1,)), ((), ())), preferred_element_type=jnp.float32
    )


def tree_sum(values, axis):
    count = lax.axis_size(axis)
    if count & (count - 1):
        return lax.psum(values, axis)
    step = 1
    while step < count:
        values = values + lax.ppermute(values, axis, [(i, i ^ step) for i in range(count)])
        step *= 2
    return values


def gram_rows(zscores, axis):
    blocks = lax.axis_size(axis)
    rows_here = zscores.shape[0]
    columns = lax.all_to_all(zscores, axis, 1, 0, tiled=True)
    partial = cross_block(columns, columns)
    pieces = lax.all_to_all(partial, axis, 0, 0, tiled=True)
    return jnp.sum(pieces.reshape(blocks, rows_here, pieces.shape[1]), axis=0)


def shards(contacts, widths, masked_bins, row_start):
    blocks = lax.axis_size("blk")
    position = lax.axis_index("blk")
    rows_here = contacts.shape[0]
    col_count = contacts.shape[1]
    nbins = rows_here * blocks
    first_row = position * rows_here
    first_bin = row_start[0]
    window_first = col_count - 1 - (first_bin + first_row + rows_here - 1)
    radius_map = skewed_map(widths, window_first, rows_here, col_count)
    padded_rows = with_halo(contacts, (("blk", 0),), WMAX)
    padded = jnp.pad(padded_rows, ((0, 0), (WMAX, WMAX)))
    smoothed = smooth(padded, radius_map)
    local_total = diagonal_totals(smoothed, window_first)
    denominator = pair_counts(first_bin, nbins, col_count)
    expected = tree_sum(local_total, "blk") / denominator
    expected_map = skewed_map(expected, window_first, rows_here, col_count)
    hit = masked_bins[:, None] == jnp.arange(col_count, dtype=masked_bins.dtype)[None, :]
    kept_bins = jnp.where(jnp.any(hit, axis=0), 0.0, 1.0).astype(jnp.float32)
    kept_rows = lax.dynamic_slice_in_dim(kept_bins, first_bin + first_row, rows_here)
    kept_total = jnp.float32(col_count - masked_bins.shape[0])
    zscores = normalize(smoothed, expected_map, kept_rows, kept_bins, kept_total)
    return gram_rows(zscores, "blk") / kept_total


def solution(mesh):
    return jax.shard_map(
        shards,
        mesh=mesh,
        in_specs=(P(("groups", "blk"), None), P("groups"), P("groups"), P("groups")),
        out_specs=P(("groups", "blk"), None),
        check_vma=False,
    )
```

```python
import jax
import jax.numpy as jnp
from jax import lax
from jax.sharding import PartitionSpec as P

WMAX = 3


def with_halo(cells, sides, width):
    for axis, dim in sides:
        count = lax.axis_size(axis)
        head = lax.slice_in_dim(cells, 0, width, axis=dim)
        tail = lax.slice_in_dim(cells, cells.shape[dim] - width, cells.shape[dim], axis=dim)
        if count % 2:
            ends = count - 1
            before = lax.ppermute(tail, axis, [(i, (i + 1) % count) for i in range(ends)])
            after = lax.ppermute(head, axis, [((i + 1) % count, i) for i in range(ends)])
        else:
            odd = lax.axis_index(axis) % 2 == 1
            inner = lax.ppermute(
                jnp.where(odd, head, tail), axis, [(i, i ^ 1) for i in range(count)]
            )
            outer = lax.ppermute(
                jnp.where(odd, tail, head),
                axis,
                [(i, i - 1) for i in range(2, count, 2)]
                + [(i, i + 1) for i in range(1, count - 1, 2)],
            )
            before = jnp.where(odd, inner, outer)
            after = jnp.where(odd, outer, inner)
        cells = jnp.concatenate([before, cells, after], axis=dim)
    return cells


def smooth(padded, radius_map):
    rows_here = padded.shape[0] - 2 * WMAX
    col_count = padded.shape[1] - 2 * WMAX
    row_sums = padded[WMAX : WMAX + rows_here]
    smoothed = jnp.zeros((rows_here, col_count), jnp.float32)
    for radius in range(WMAX + 1):
        if radius > 0:
            row_sums = (
                row_sums
                + padded[WMAX - radius : WMAX - radius + rows_here]
                + padded[WMAX + radius : WMAX + radius + rows_here]
            )
        box_sums = row_sums[:, WMAX : WMAX + col_count]
        for offset in range(1, radius + 1):
            box_sums = (
                box_sums
                + row_sums[:, WMAX - offset : WMAX - offset + col_count]
                + row_sums[:, WMAX + offset : WMAX + offset + col_count]
            )
        smoothed = smoothed + jnp.where(
            radius_map == radius, box_sums / float((2 * radius + 1) ** 2), 0.0
        )
    return smoothed


def pair_counts(first_bin, nrows, col_count):
    distance = jnp.arange(col_count, dtype=jnp.int32)
    upper_pairs = jnp.clip(col_count - distance - first_bin, 0, nrows)
    lower_pairs = jnp.clip(first_bin + nrows - distance, 0, nrows)
    pair_total = jnp.where(distance == 0, nrows, upper_pairs + lower_pairs)
    return jnp.maximum(pair_total, 1).astype(jnp.float32)


def mirrored_table(table, margin=0):
    mirrored = jnp.concatenate([table[1:][::-1], table])
    return jnp.pad(mirrored, margin, mode="edge")


def skewed_map(table, window_first, rows_here, col_count, margin=0):
    span = col_count + rows_here - 1
    window = lax.dynamic_slice_in_dim(
        mirrored_table(table, margin), window_first + margin, span
    )
    tiled = jnp.tile(window, rows_here + 1)
    flat = tiled[rows_here - 1 : rows_here - 1 + rows_here * (span - 1)]
    return flat.reshape(rows_here, span - 1)[:, :col_count]


def diagonal_totals(smoothed, window_first, margin=0):
    rows_here = smoothed.shape[0]
    col_count = smoothed.shape[1]
    span = col_count + rows_here - 1
    placed = jnp.pad(smoothed, ((0, 0), (rows_here - 1, 0)))
    flat = jnp.pad(placed.reshape(rows_here * span), (0, rows_here))
    offsets = jnp.sum(flat.reshape(rows_here, span + 1), axis=0)[:span]
    spread = lax.dynamic_update_slice_in_dim(
        jnp.zeros((2 * col_count - 1 + 2 * margin,), jnp.float32),
        offsets,
        window_first + margin,
        0,
    )[margin : margin + 2 * col_count - 1]
    lower = jnp.concatenate([jnp.zeros((1,), jnp.float32), spread[: col_count - 1][::-1]])
    return spread[col_count - 1 :] + lower


def normalize(smoothed, expected_map, kept_rows, kept_cols, kept_total):
    ratio = smoothed / expected_map
    row_mean = jnp.sum(ratio * kept_cols[None, :], axis=1, keepdims=True) / kept_total
    centred = (ratio - row_mean) * kept_cols[None, :]
    variance = jnp.sum(centred * centred, axis=1, keepdims=True) / kept_total
    return (centred * lax.rsqrt(variance + 1e-05) * kept_rows[:, None]).astype(jnp.bfloat16)


def cross_block(left, right):
    return lax.dot_general(
        left, right, (((1,), (1,)), ((), ())), preferred_element_type=jnp.float32
    )


def tree_sum(values, axis):
    count = lax.axis_size(axis)
    if count & (count - 1):
        return lax.psum(values, axis)
    step = 1
    while step < count:
        values = values + lax.ppermute(values, axis, [(i, i ^ step) for i in range(count)])
        step *= 2
    return values


def gram_rows(zscores, axis):
    blocks = lax.axis_size(axis)
    rows_here = zscores.shape[0]
    columns = lax.all_to_all(zscores, axis, 1, 0, tiled=True)
    partial = cross_block(columns, columns)
    pieces = lax.all_to_all(partial, axis, 0, 0, tiled=True)
    return jnp.sum(pieces.reshape(blocks, rows_here, pieces.shape[1]), axis=0)


def shards(contacts, widths, masked_bins, row_start):
    blocks = lax.axis_size("blk")
    position = lax.axis_index("blk")
    rows_here = contacts.shape[0]
    col_count = contacts.shape[1]
    nbins = rows_here * blocks
    first_row = position * rows_here
    first_bin = row_start[0]
    window_first = col_count - 1 - (first_bin + first_row + rows_here - 1)
    wide_rows = rows_here + 2 * WMAX
    wide_first = window_first - WMAX
    wide_radius = skewed_map(widths, wide_first, wide_rows, col_count, WMAX)
    own = jnp.pad(contacts, ((2 * WMAX, 2 * WMAX), (WMAX, WMAX)))
    target = first_row - WMAX + jnp.arange(wide_rows, dtype=jnp.int32)
    inside = (target >= 0) & (target < nbins)
    own_part = jnp.where(inside[:, None], smooth(own, wide_radius), 0.0)
    local_total = diagonal_totals(own_part, wide_first, WMAX)
    radius_map = skewed_map(widths, window_first, rows_here, col_count)
    padded_rows = with_halo(contacts, (("blk", 0),), WMAX)
    padded = jnp.pad(padded_rows, ((0, 0), (WMAX, WMAX)))
    smoothed = lax.optimization_barrier(smooth(padded, radius_map))
    denominator = pair_counts(first_bin, nbins, col_count)
    expected = tree_sum(local_total, "blk") / denominator
    expected_map = skewed_map(expected, window_first, rows_here, col_count)
    kept_bins = jnp.ones((col_count,), jnp.float32).at[masked_bins].set(0.0)
    kept_rows = lax.dynamic_slice_in_dim(kept_bins, first_bin + first_row, rows_here)
    kept_total = jnp.float32(col_count - masked_bins.shape[0])
    zscores = normalize(smoothed, expected_map, kept_rows, kept_bins, kept_total)
    return gram_rows(zscores, "blk") / kept_total


def solution(mesh):
    return jax.shard_map(
        shards,
        mesh=mesh,
        in_specs=(P(("groups", "blk"), None), P("groups"), P("groups"), P("groups")),
        out_specs=P(("groups", "blk"), None),
        check_vma=False,
    )
```

```python
import jax
import jax.numpy as jnp
from jax import lax
from jax.sharding import PartitionSpec as P

WMAX = 3


def with_halo(cells, sides, width):
    for axis, dim in sides:
        count = lax.axis_size(axis)
        head = lax.slice_in_dim(cells, 0, width, axis=dim)
        tail = lax.slice_in_dim(cells, cells.shape[dim] - width, cells.shape[dim], axis=dim)
        if count % 2:
            ends = count - 1
            before = lax.ppermute(tail, axis, [(i, (i + 1) % count) for i in range(ends)])
            after = lax.ppermute(head, axis, [((i + 1) % count, i) for i in range(ends)])
        else:
            odd = lax.axis_index(axis) % 2 == 1
            inner = lax.ppermute(
                jnp.where(odd, head, tail), axis, [(i, i ^ 1) for i in range(count)]
            )
            outer = lax.ppermute(
                jnp.where(odd, tail, head),
                axis,
                [(i, i - 1) for i in range(2, count, 2)]
                + [(i, i + 1) for i in range(1, count - 1, 2)],
            )
            before = jnp.where(odd, inner, outer)
            after = jnp.where(odd, outer, inner)
        cells = jnp.concatenate([before, cells, after], axis=dim)
    return cells


def smooth(padded, radius_map):
    rows_here = padded.shape[0] - 2 * WMAX
    col_count = padded.shape[1] - 2 * WMAX
    row_sums = padded[WMAX : WMAX + rows_here]
    smoothed = jnp.zeros((rows_here, col_count), jnp.float32)
    for radius in range(WMAX + 1):
        if radius > 0:
            row_sums = (
                row_sums
                + padded[WMAX - radius : WMAX - radius + rows_here]
                + padded[WMAX + radius : WMAX + radius + rows_here]
            )
        box_sums = row_sums[:, WMAX : WMAX + col_count]
        for offset in range(1, radius + 1):
            box_sums = (
                box_sums
                + row_sums[:, WMAX - offset : WMAX - offset + col_count]
                + row_sums[:, WMAX + offset : WMAX + offset + col_count]
            )
        smoothed = smoothed + jnp.where(
            radius_map == radius, box_sums / float((2 * radius + 1) ** 2), 0.0
        )
    return smoothed


def pair_counts(first_bin, nrows, col_count):
    distance = jnp.arange(col_count, dtype=jnp.int32)
    upper_pairs = jnp.clip(col_count - distance - first_bin, 0, nrows)
    lower_pairs = jnp.clip(first_bin + nrows - distance, 0, nrows)
    pair_total = jnp.where(distance == 0, nrows, upper_pairs + lower_pairs)
    return jnp.maximum(pair_total, 1).astype(jnp.float32)


def mirrored_table(table):
    return jnp.concatenate([table[1:][::-1], table])


def skewed_map(table, window_first, rows_here, col_count):
    span = col_count + rows_here - 1
    window = lax.dynamic_slice_in_dim(mirrored_table(table), window_first, span)
    tiled = jnp.tile(window, rows_here + 1)
    flat = tiled[rows_here - 1 : rows_here - 1 + rows_here * (span - 1)]
    return flat.reshape(rows_here, span - 1)[:, :col_count]


def diagonal_totals(smoothed, window_first):
    rows_here = smoothed.shape[0]
    col_count = smoothed.shape[1]
    span = col_count + rows_here - 1
    placed = jnp.pad(smoothed, ((0, 0), (rows_here - 1, 0)))
    flat = jnp.pad(placed.reshape(rows_here * span), (0, rows_here))
    offsets = jnp.sum(flat.reshape(rows_here, span + 1), axis=0)[:span]
    spread = lax.dynamic_update_slice_in_dim(
        jnp.zeros((2 * col_count - 1,), jnp.float32), offsets, window_first, 0
    )
    lower = jnp.concatenate([jnp.zeros((1,), jnp.float32), spread[: col_count - 1][::-1]])
    return spread[col_count - 1 :] + lower


def normalize(smoothed, expected_map, kept_rows, kept_cols, kept_total):
    ratio = smoothed / expected_map
    row_mean = jnp.sum(ratio * kept_cols[None, :], axis=1, keepdims=True) / kept_total
    centred = (ratio - row_mean) * kept_cols[None, :]
    variance = jnp.sum(centred * centred, axis=1, keepdims=True) / kept_total
    return (centred * lax.rsqrt(variance + 1e-05) * kept_rows[:, None]).astype(jnp.bfloat16)


def cross_block(left, right):
    return lax.dot_general(
        left, right, (((1,), (1,)), ((), ())), preferred_element_type=jnp.float32
    )


def tree_sum(values, axis):
    count = lax.axis_size(axis)
    if count & (count - 1):
        return lax.psum(values, axis)
    step = 1
    while step < count:
        values = values + lax.ppermute(values, axis, [(i, i ^ step) for i in range(count)])
        step *= 2
    return values


def gram_rows(zscores, axis):
    blocks = lax.axis_size(axis)
    rows_here = zscores.shape[0]
    columns = lax.all_to_all(zscores, axis, 1, 0, tiled=True)
    partial = cross_block(columns, columns)
    pieces = lax.all_to_all(partial, axis, 0, 0, tiled=True)
    return jnp.sum(pieces.reshape(blocks, rows_here, pieces.shape[1]), axis=0)


def shards(contacts, widths, masked_bins, row_start):
    blocks = lax.axis_size("blk")
    position = lax.axis_index("blk")
    rows_here = contacts.shape[0]
    col_count = contacts.shape[1]
    nbins = rows_here * blocks
    first_row = position * rows_here
    first_bin = row_start[0]
    window_first = col_count - 1 - (first_bin + first_row + rows_here - 1)
    radius_map = skewed_map(widths, window_first, rows_here, col_count)
    own = lax.optimization_barrier(jnp.pad(contacts, WMAX))
    halo = with_halo(own[WMAX:-WMAX, WMAX:-WMAX], (("blk", 0),), WMAX)
    top = jnp.pad(halo[:WMAX], ((0, rows_here + WMAX), (WMAX, WMAX)))
    bottom = jnp.pad(halo[-WMAX:], ((rows_here + WMAX, 0), (WMAX, WMAX)))
    row = lax.broadcasted_iota(jnp.int32, own.shape, 0)
    padded = jnp.where(row < WMAX, top, jnp.where(row >= rows_here + WMAX, bottom, own))
    smoothed = smooth(padded, radius_map)
    local_total = diagonal_totals(smoothed, window_first)
    denominator = pair_counts(first_bin, nbins, col_count)
    expected = tree_sum(local_total, "blk") / denominator
    expected_map = skewed_map(expected, window_first, rows_here, col_count)
    kept_bins = jnp.ones((col_count,), jnp.float32).at[masked_bins].set(0.0)
    kept_rows = lax.dynamic_slice_in_dim(kept_bins, first_bin + first_row, rows_here)
    kept_total = jnp.float32(col_count - masked_bins.shape[0])
    zscores = normalize(smoothed, expected_map, kept_rows, kept_bins, kept_total)
    return gram_rows(zscores, "blk") / kept_total


def solution(mesh):
    return jax.shard_map(
        shards,
        mesh=mesh,
        in_specs=(P(("groups", "blk"), None), P("groups"), P("groups"), P("groups")),
        out_specs=P(("groups", "blk"), None),
        check_vma=False,
    )
```

```python
import jax
import jax.numpy as jnp
from jax import lax
from jax.sharding import PartitionSpec as P

WMAX = 3


def with_halo(cells, sides, width):
    for axis, dim in sides:
        count = lax.axis_size(axis)
        head = lax.slice_in_dim(cells, 0, width, axis=dim)
        tail = lax.slice_in_dim(cells, cells.shape[dim] - width, cells.shape[dim], axis=dim)
        if count % 2:
            ends = count - 1
            before = lax.ppermute(tail, axis, [(i, (i + 1) % count) for i in range(ends)])
            after = lax.ppermute(head, axis, [((i + 1) % count, i) for i in range(ends)])
        else:
            odd = lax.axis_index(axis) % 2 == 1
            inner = lax.ppermute(
                jnp.where(odd, head, tail), axis, [(i, i ^ 1) for i in range(count)]
            )
            outer = lax.ppermute(
                jnp.where(odd, tail, head),
                axis,
                [(i, i - 1) for i in range(2, count, 2)]
                + [(i, i + 1) for i in range(1, count - 1, 2)],
            )
            before = jnp.where(odd, inner, outer)
            after = jnp.where(odd, outer, inner)
        cells = jnp.concatenate([before, cells, after], axis=dim)
    return cells


def smooth(padded, radius_map):
    rows_here = padded.shape[0] - 2 * WMAX
    col_count = padded.shape[1] - 2 * WMAX
    row_sums = padded[WMAX : WMAX + rows_here]
    smoothed = jnp.zeros((rows_here, col_count), jnp.float32)
    for radius in range(WMAX + 1):
        if radius > 0:
            row_sums = (
                row_sums
                + padded[WMAX - radius : WMAX - radius + rows_here]
                + padded[WMAX + radius : WMAX + radius + rows_here]
            )
        box_sums = row_sums[:, WMAX : WMAX + col_count]
        for offset in range(1, radius + 1):
            box_sums = (
                box_sums
                + row_sums[:, WMAX - offset : WMAX - offset + col_count]
                + row_sums[:, WMAX + offset : WMAX + offset + col_count]
            )
        smoothed = smoothed + jnp.where(
            radius_map == radius, box_sums / float((2 * radius + 1) ** 2), 0.0
        )
    return smoothed


def pair_counts(first_bin, nrows, col_count):
    distance = jnp.arange(col_count, dtype=jnp.int32)
    upper_pairs = jnp.clip(col_count - distance - first_bin, 0, nrows)
    lower_pairs = jnp.clip(first_bin + nrows - distance, 0, nrows)
    pair_total = jnp.where(distance == 0, nrows, upper_pairs + lower_pairs)
    return jnp.maximum(pair_total, 1).astype(jnp.float32)


def mirrored_table(table):
    return jnp.concatenate([table[1:][::-1], table])


def skewed_map(table, window_first, rows_here, col_count):
    span = col_count + rows_here - 1
    window = lax.dynamic_slice_in_dim(mirrored_table(table), window_first, span)
    tiled = jnp.tile(window, rows_here + 1)
    flat = tiled[rows_here - 1 : rows_here - 1 + rows_here * (span - 1)]
    return flat.reshape(rows_here, span - 1)[:, :col_count]


def diagonal_totals(smoothed, window_first):
    rows_here = smoothed.shape[0]
    col_count = smoothed.shape[1]
    span = col_count + rows_here - 1
    placed = jnp.pad(smoothed, ((0, 0), (rows_here - 1, 0)))
    flat = jnp.pad(placed.reshape(rows_here * span), (0, rows_here))
    offsets = jnp.sum(flat.reshape(rows_here, span + 1), axis=0)[:span]
    spread = lax.dynamic_update_slice_in_dim(
        jnp.zeros((2 * col_count - 1,), jnp.float32), offsets, window_first, 0
    )
    lower = jnp.concatenate([jnp.zeros((1,), jnp.float32), spread[: col_count - 1][::-1]])
    return spread[col_count - 1 :] + lower


def normalize(smoothed, expected_map, kept_rows, kept_cols, kept_total):
    ratio = smoothed / expected_map
    row_mean = jnp.sum(ratio * kept_cols[None, :], axis=1, keepdims=True) / kept_total
    centred = (ratio - row_mean) * kept_cols[None, :]
    variance = jnp.sum(centred * centred, axis=1, keepdims=True) / kept_total
    return (centred * lax.rsqrt(variance + 1e-05) * kept_rows[:, None]).astype(jnp.bfloat16)


def cross_block(left, right):
    return lax.dot_general(
        left, right, (((1,), (1,)), ((), ())), preferred_element_type=jnp.float32
    )


def tree_sum(values, axis):
    count = lax.axis_size(axis)
    if count & (count - 1):
        return lax.psum(values, axis)
    step = 1
    while step < count:
        values = values + lax.ppermute(values, axis, [(i, i ^ step) for i in range(count)])
        step *= 2
    return values


def gram_rows(zscores, axis, scale):
    blocks = lax.axis_size(axis)
    rows_here = zscores.shape[0]
    columns = lax.all_to_all(zscores, axis, 1, 0, tiled=True)
    partial = cross_block(columns, columns) / scale
    pieces = lax.all_to_all(partial, axis, 0, 0, tiled=True)
    return jnp.sum(pieces.reshape(blocks, rows_here, pieces.shape[1]), axis=0)


def shards(contacts, widths, masked_bins, row_start):
    blocks = lax.axis_size("blk")
    position = lax.axis_index("blk")
    rows_here = contacts.shape[0]
    col_count = contacts.shape[1]
    nbins = rows_here * blocks
    first_row = position * rows_here
    first_bin = row_start[0]
    window_first = col_count - 1 - (first_bin + first_row + rows_here - 1)
    radius_map = skewed_map(widths, window_first, rows_here, col_count)
    own = lax.optimization_barrier(jnp.pad(contacts, WMAX))
    halo = with_halo(own[WMAX:-WMAX, WMAX:-WMAX], (("blk", 0),), WMAX)
    top = jnp.pad(halo[:WMAX], ((0, rows_here + WMAX), (WMAX, WMAX)))
    bottom = jnp.pad(halo[-WMAX:], ((rows_here + WMAX, 0), (WMAX, WMAX)))
    row = lax.broadcasted_iota(jnp.int32, own.shape, 0)
    padded = jnp.where(row < WMAX, top, jnp.where(row >= rows_here + WMAX, bottom, own))
    smoothed = smooth(padded, radius_map)
    local_total = diagonal_totals(smoothed, window_first)
    denominator = pair_counts(first_bin, nbins, col_count)
    expected = tree_sum(local_total, "blk") / denominator
    expected_map = skewed_map(expected, window_first, rows_here, col_count)
    hit = masked_bins[:, None] == jnp.arange(col_count, dtype=masked_bins.dtype)[None, :]
    kept_bins = jnp.where(jnp.any(hit, axis=0), 0.0, 1.0).astype(jnp.float32)
    kept_rows = lax.dynamic_slice_in_dim(kept_bins, first_bin + first_row, rows_here)
    kept_total = jnp.float32(col_count - masked_bins.shape[0])
    zscores = normalize(smoothed, expected_map, kept_rows, kept_bins, kept_total)
    return gram_rows(zscores, "blk", kept_total)


def solution(mesh):
    return jax.shard_map(
        shards,
        mesh=mesh,
        in_specs=(P(("groups", "blk"), None), P("groups"), P("groups"), P("groups")),
        out_specs=P(("groups", "blk"), None),
        check_vma=False,
    )
```
